32 devices in a mesh: kv: 4 (over z), blk: 8 (over y, x, core).
Axes of the slice: x: 2, y: 2, z: 4, core: 2. Of those that a mesh axis runs over, the one named last changes fastest.
Arguments:
- queries: bfloat16 [640, 2048], P('blk', 'kv'), may hold values from -32 to 32, as said below
- keys: bfloat16 [640, 512], P('blk', 'kv'), may hold values from -7 to 7, as said below
- values: bfloat16 [640, 512], P('blk', 'kv'), may hold values from -6 to 6
- lengths: int32 [4], replicated, may hold values from 1 to 80, 128 in all
- out_weight: bfloat16 [4096, 2048], P('blk', 'kv'), may hold values from -0.125 to 0.125
Outputs:
- hidden: bfloat16 [640, 4096], P('blk', 'kv')
- cache_keys: bfloat16 [640, 512], P('blk', 'kv')
The draws below stay inside these ranges and needn't reach their ends.
Inputs may be any that keep to these rules, and one draw needn't show every extreme that they name: `queries`: rotary inputs of order one; in some rows a query head may be a multiple of its key head. `keys`: key projections of order one. `lengths`: each short prompt is 1 to 80 tokens long, one of them exactly 80; their sum is 128.
All inputs are finite; a program needn't handle non-finite values.
Results may differ from the reference program's by a relative error of at most 0.0095.
Values may be sent and summed in bfloat16 or wider, within the bound.
No kernel may reach another device: no remote copies, remote signals or barrier semaphores. Data moves between devices by JAX's collectives and lax.ppermute only.
A program may use at most 64 MiB of HBM per device.

```python
import math
import jax
import jax.numpy as jnp
import numpy as np
from jax import lax

D = 4096
HD = 128
KVH = 4
QPG = 4
TOK_DEV = 80
TOKENS = 640
LONG = 512
SHORTS = 4
HQ = 16


def draw_pair(key):
    key_rows = jax.random.normal(jax.random.fold_in(key, 11), (TOKENS, KVH * HD), jnp.float32)
    key_rows = jnp.clip(key_rows, -6.0, 6.0)
    query_rows = 2.0 * jax.random.normal(jax.random.fold_in(key, 12), (TOKENS, KVH * QPG * HD), jnp.float32)
    query_rows = jnp.clip(query_rows, -12.0, 12.0)
    return (query_rows, key_rows)


def draw_queries(key, part):
    return draw_pair(key)[0].astype(jnp.bfloat16)


def draw_keys(key, part):
    return draw_pair(key)[1].astype(jnp.bfloat16)


def levels(rng, dims, cuts, least, high):
    def one(dim, shards_of):
        draws = jax.random.uniform(jax.random.fold_in(jax.random.fold_in(rng, 6), dim), (shards_of,), jnp.float32, least / len(cuts), high / len(cuts))
        return jnp.repeat(jnp.exp(draws), dims[dim] // shards_of).reshape((-1,) + (1,) * (len(dims) - dim - 1))

    factor_of = one(*cuts[0])
    for cut in cuts[1:]:
        factor_of = factor_of * one(*cut)
    return factor_of


def length_profile(count, total, reach, lean):
    loads = [(1 << 20) // math.isqrt(standing ** lean) + 1 for standing in range(2, count + 1)]
    spare, holding = total - reach - (count - 1), [1] * (count - 1)
    while spare > 0:
        candidates = [i for i in range(count - 1) if holding[i] < reach]
        whole, left = sum([loads[i] for i in candidates]), spare
        for i in candidates:
            addition = min(reach - holding[i], max(1, left * loads[i] // whole), spare)
            holding[i] = holding[i] + addition
            spare = spare - addition
    return np.array([reach] + holding)


def ragged_sizes(stream_key, count, total, reach, skew):
    if count == 2:
        one = jax.random.randint(stream_key, (), max(1, total - reach), min(reach, total - 1) + 1)
        return jnp.stack([one, total - one])
    sizes = jnp.asarray(length_profile(count, total, reach, skew), jnp.int32)
    pairs = (count - 1) // 2
    source_of, sink = sizes[1:1 + 2 * pairs:2], sizes[2:2 + 2 * pairs:2]
    room = jnp.minimum(source_of - 1, reach - sink)
    moved = jax.random.randint(jax.random.fold_in(stream_key, 1), (pairs,), 0, 1 << 20) % (room + 1)
    sizes = sizes.at[1:1 + 2 * pairs:2].set(source_of - moved).at[2:2 + 2 * pairs:2].set(sink + moved)
    return sizes[jax.random.permutation(jax.random.fold_in(stream_key, 2), count)]


def normal_values(stream_key, shape, scale, reach, shards=(), dtype=jnp.bfloat16):
    gain = levels(stream_key, shape, shards, -0.22, 0.18) if shards else 1.0
    array = jax.random.normal(stream_key, shape, jnp.float32) * scale * gain
    return jnp.minimum(jnp.maximum(array, -reach), reach).astype(dtype)


def setup_inputs(seed: int = 0) -> dict:
    arg_keys = jax.random.split(jax.random.key(seed), 6)
    queries = draw_queries(jax.random.fold_in(arg_keys[5], 71), 0)
    keys = draw_keys(jax.random.fold_in(arg_keys[5], 71), 0)
    values = normal_values(arg_keys[2], (TOKENS, KVH * HD), 1.0, 6.0, ((0, 8), (1, 4)))
    lengths = ragged_sizes(arg_keys[3], SHORTS, TOKENS - LONG, TOK_DEV, 2).astype(jnp.int32)
    out_weight = normal_values(arg_keys[4], (D, HQ * HD), (HQ * HD) ** -0.5, 0.125, ((0, 8), (1, 4)))
    return {"queries": queries, "keys": keys, "values": values, "lengths": lengths, "out_weight": out_weight}


rope_base = 500000.0


def locate(index, starts):
    hit = starts[None, :] <= index[:, None]
    segment = (jnp.sum(hit.astype(jnp.int32), axis=1) - 1).astype(jnp.int32)
    offset = jnp.max(jnp.where(hit, starts[None, :], 0), axis=1).astype(jnp.int32)
    return segment, offset


def rotate(field, positions):
    half = field.shape[-1] // 2
    steps = jnp.arange(half).astype(jnp.float32) * (2.0 / field.shape[-1])
    inverse = jnp.power(jnp.float32(rope_base), -steps)
    angle = positions.astype(jnp.float32)[:, None, None] * inverse[None, None, :]
    cosine = jnp.cos(angle)
    sine = jnp.sin(angle)
    first = field[..., :half].astype(jnp.float32)
    second = field[..., half:].astype(jnp.float32)
    return jnp.concatenate([first * cosine - second * sine, second * cosine + first * sine], axis=-1)


def reference(queries, keys, values, lengths, out_weight):
    total_len = queries.shape[0]
    long_len = total_len - jnp.sum(lengths)
    shifted = jnp.concatenate([jnp.zeros((1,), jnp.int32), jnp.cumsum(lengths)[:-1].astype(jnp.int32)])
    starts = jnp.concatenate([jnp.zeros((1,), jnp.int32), (long_len + shifted).astype(jnp.int32)])
    index = jnp.arange(total_len).astype(jnp.int32)
    segment, offset = locate(index, starts)
    positions = index - offset
    rot_keys = rotate(keys.reshape(total_len, KVH, HD), positions).astype(jnp.bfloat16)
    rot_queries = rotate(queries.reshape(total_len, HQ, HD), positions).astype(jnp.bfloat16)
    scale = 1.0 / (HD ** 0.5)
    keys_wide = rot_keys.astype(jnp.float32)
    values_wide = values.reshape(total_len, KVH, HD).astype(jnp.float32)
    count = total_len // TOK_DEV

    def attend(block_idx):
        begin = (block_idx * TOK_DEV).astype(jnp.int32)
        query_blk = lax.dynamic_slice_in_dim(rot_queries, begin, TOK_DEV, 0).astype(jnp.float32)
        query_idx = lax.dynamic_slice_in_dim(index, begin, TOK_DEV, 0)
        query_seg = lax.dynamic_slice_in_dim(segment, begin, TOK_DEV, 0)
        live = (segment[None, :] == query_seg[:, None]) & (index[None, :] <= query_idx[:, None])
        pieces = []
        for group in range(KVH):
            group_q = query_blk[:, group * QPG:(group + 1) * QPG]
            scores = jnp.einsum("bhd,nd->bhn", group_q, keys_wide[:, group]) * scale
            scores = jnp.where(live[:, None, :], scores, -1e30)
            row_max = jnp.max(scores, axis=2, keepdims=True)
            expo = jnp.where(live[:, None, :], jnp.exp(scores - row_max), 0.0)
            row_sum = jnp.sum(expo, axis=2, keepdims=True)
            rounded = expo.astype(jnp.bfloat16).astype(jnp.float32)
            weighted = jnp.einsum("bhn,nd->bhd", rounded, values_wide[:, group])
            pieces.append((weighted / row_sum).astype(jnp.bfloat16).reshape(TOK_DEV, QPG * HD))
        return jnp.concatenate(pieces, axis=1)

    attended = lax.map(attend, jnp.arange(count).astype(jnp.int32)).reshape(total_len, HQ * HD)
    width = QPG * HD
    hidden = jnp.zeros((total_len, out_weight.shape[0]), jnp.float32)
    for group in range(KVH):
        part_att = attended[:, group * width:(group + 1) * width]
        part_w = out_weight[:, group * width:(group + 1) * width]
        partial_value = jnp.dot(part_att, part_w.T, preferred_element_type=jnp.float32).astype(jnp.bfloat16)
        partial_value = lax.optimization_barrier(partial_value)
        hidden = hidden + partial_value.astype(jnp.float32)
    return hidden.astype(jnp.bfloat16), rot_keys.reshape(total_len, KVH * HD)
```

```python
import jax
import jax.numpy as jnp
from jax import lax
from jax.sharding import Mesh
from jax.sharding import PartitionSpec as P

rope_base = 500000.0
BLK = ("chip", "core")


def locate(index, starts):
    hit = starts[None, :] <= index[:, None]
    segment = jnp.sum(hit.astype(jnp.int32), axis=1) - 1
    offset = jnp.max(jnp.where(hit, starts[None, :], 0), axis=1)
    return (segment, offset)


def rotate(field, positions):
    half = field.shape[-1] // 2
    steps = jnp.arange(half).astype(jnp.float32) * (2.0 / field.shape[-1])
    inverse = jnp.power(jnp.float32(rope_base), -steps)
    angle = positions.astype(jnp.float32)[:, None, None] * inverse[None, None, :]
    cosine = jnp.cos(angle)
    sine = jnp.sin(angle)
    first = field[..., :half].astype(jnp.float32)
    second = field[..., half:].astype(jnp.float32)
    return jnp.concatenate(
        [first * cosine - second * sine, second * cosine + first * sine], axis=-1
    )


def body(queries, keys, values, lengths, out_weight):
    tok_rows = queries.shape[0]
    head_size = keys.shape[1]
    groups = queries.shape[1] // head_size
    cores = lax.axis_size("core")
    total_len = tok_rows * lax.axis_size("chip") * cores
    long_len = total_len - jnp.sum(lengths)
    shifted = jnp.concatenate([jnp.zeros((1,), jnp.int32), jnp.cumsum(lengths)[:-1]])
    starts = jnp.concatenate([jnp.zeros((1,), jnp.int32), long_len + shifted])
    blk_idx = lax.axis_index("chip") * cores + lax.axis_index("core")
    first_tok = blk_idx * tok_rows
    query_idx = first_tok + jnp.arange(tok_rows)
    query_seg, query_off = locate(query_idx, starts)
    positions = query_idx - query_off
    rot_keys = (
        rotate(keys.reshape(tok_rows, 1, head_size), positions)
        .astype(jnp.bfloat16)
        .reshape(tok_rows, head_size)
    )
    rot_queries = rotate(queries.reshape(tok_rows, groups, head_size), positions).astype(
        jnp.bfloat16
    )
    w_share = lax.all_gather(out_weight, "chip", axis=0, tiled=True)
    query_rows = jnp.transpose(rot_queries, (1, 0, 2)).reshape(groups * tok_rows, head_size)
    row_idx = jnp.tile(query_idx, groups)
    row_seg = jnp.tile(query_seg, groups)
    scale = 1.0 / head_size**0.5
    kv_pair = lax.all_gather(
        jnp.concatenate([rot_keys, values], axis=1), BLK, axis=0, tiled=True
    )
    key_piece = kv_pair[:, :head_size]
    value_piece = kv_pair[:, head_size:]
    span = key_piece.shape[0]
    key_idx = jnp.arange(span)
    key_seg, key_off = locate(key_idx, starts)
    live = (key_seg[None, :] == row_seg[:, None]) & (key_idx[None, :] <= row_idx[:, None])
    scores = (
        jnp.einsum("rd,nd->rn", query_rows, key_piece, preferred_element_type=jnp.float32) * scale
    )
    scores = jnp.where(live, scores, -1e30)
    new_max = jnp.max(scores, axis=1)
    probs = jnp.where(live, jnp.exp(scores - new_max[:, None]), 0.0)
    new_sum = jnp.sum(probs, axis=1)
    new_weighted = jnp.dot(
        probs.astype(jnp.bfloat16), value_piece, preferred_element_type=jnp.float32
    )
    attended = (new_weighted / new_sum[:, None]).astype(jnp.bfloat16)
    attended = jnp.transpose(attended.reshape(groups, tok_rows, head_size), (1, 0, 2)).reshape(
        tok_rows, groups * head_size
    )
    chip_att = lax.all_gather(attended, "core", axis=0, tiled=True)
    terms = jnp.einsum(
        "tk,nk->tn", chip_att, w_share, preferred_element_type=jnp.float32
    ).astype(jnp.bfloat16)
    summed = lax.psum_scatter(terms, "kv", scatter_dimension=1, tiled=True)
    hidden = lax.all_to_all(summed, "core", 0, 1, tiled=True)
    return (hidden, rot_keys)


def solution(mesh):
    kv_size, blk_size = mesh.devices.shape
    sub = Mesh(mesh.devices.reshape(kv_size, blk_size // 2, 2), ("kv",) + BLK)
    return jax.shard_map(
        body,
        mesh=sub,
        in_specs=(P(BLK, "kv"), P(BLK, "kv"), P(BLK, "kv"), P(), P(BLK, "kv")),
        out_specs=(P(BLK, "kv"), P(BLK, "kv")),
        check_vma=False,
    )
```

```python
import jax
import jax.numpy as jnp
from jax import lax
from jax.sharding import Mesh
from jax.sharding import PartitionSpec as P

rope_base = 500000.0
BLK = ("chip", "core")


def locate(index, starts):
    hit = starts[None, :] <= index[:, None]
    segment = jnp.sum(hit.astype(jnp.int32), axis=1) - 1
    offset = jnp.max(jnp.where(hit, starts[None, :], 0), axis=1)
    return (segment, offset)


def rotate(field, positions):
    half = field.shape[-1] // 2
    steps = jnp.arange(half).astype(jnp.float32) * (2.0 / field.shape[-1])
    inverse = jnp.power(jnp.float32(rope_base), -steps)
    angle = positions.astype(jnp.float32)[:, None, None] * inverse[None, None, :]
    cosine = jnp.cos(angle)
    sine = jnp.sin(angle)
    first = field[..., :half].astype(jnp.float32)
    second = field[..., half:].astype(jnp.float32)
    return jnp.concatenate(
        [first * cosine - second * sine, second * cosine + first * sine], axis=-1
    )


def body(queries, keys, values, lengths, out_weight):
    tok_rows = queries.shape[0]
    head_size = keys.shape[1]
    groups = queries.shape[1] // head_size
    cores = lax.axis_size("core")
    total_len = tok_rows * lax.axis_size("chip") * cores
    long_len = total_len - jnp.sum(lengths)
    shifted = jnp.concatenate([jnp.zeros((1,), jnp.int32), jnp.cumsum(lengths)[:-1]])
    starts = jnp.concatenate([jnp.zeros((1,), jnp.int32), long_len + shifted])
    blk_idx = lax.axis_index("chip") * cores + lax.axis_index("core")
    first_tok = blk_idx * tok_rows
    query_idx = first_tok + jnp.arange(tok_rows)
    query_seg, query_off = locate(query_idx, starts)
    positions = query_idx - query_off
    rot_keys = (
        rotate(keys.reshape(tok_rows, 1, head_size), positions)
        .astype(jnp.bfloat16)
        .reshape(tok_rows, head_size)
    )
    rot_queries = rotate(queries.reshape(tok_rows, groups, head_size), positions).astype(
        jnp.bfloat16
    )
    chips = lax.axis_size("chip")
    if chips <= 8:
        held = [out_weight] + [
            lax.ppermute(out_weight, "chip", [(i, (i + s) % chips) for i in range(chips)])
            for s in range(1, chips)
        ]
        back = jnp.stack(held[::-1] + held[::-1], axis=0)
        here = lax.axis_index("chip")
        w_share = lax.dynamic_slice_in_dim(back, chips - 1 - here, chips, 0).reshape(
            chips * out_weight.shape[0], out_weight.shape[1]
        )
    else:
        w_share = lax.all_gather(out_weight, "chip", axis=0, tiled=True)
    query_rows = jnp.transpose(rot_queries, (1, 0, 2)).reshape(groups * tok_rows, head_size)
    row_idx = jnp.tile(query_idx, groups)
    row_seg = jnp.tile(query_seg, groups)
    scale = 1.0 / head_size**0.5
    kv_pair = lax.all_gather(
        jnp.concatenate([rot_keys, values], axis=1), BLK, axis=0, tiled=True
    )
    key_piece = kv_pair[:, :head_size]
    value_piece = kv_pair[:, head_size:]
    span = key_piece.shape[0]
    key_idx = jnp.arange(span)
    key_seg, key_off = locate(key_idx, starts)
    live = (key_seg[None, :] == row_seg[:, None]) & (key_idx[None, :] <= row_idx[:, None])
    scores = (
        jnp.einsum("rd,nd->rn", query_rows, key_piece, preferred_element_type=jnp.float32) * scale
    )
    scores = jnp.where(live, scores, -1e30)
    new_max = jnp.max(scores, axis=1)
    probs = jnp.where(live, jnp.exp(scores - new_max[:, None]), 0.0)
    new_sum = jnp.sum(probs, axis=1)
    new_weighted = jnp.dot(
        probs.astype(jnp.bfloat16), value_piece, preferred_element_type=jnp.float32
    )
    attended = (new_weighted / new_sum[:, None]).astype(jnp.bfloat16)
    attended = jnp.transpose(attended.reshape(groups, tok_rows, head_size), (1, 0, 2)).reshape(
        tok_rows, groups * head_size
    )
    chip_att = lax.all_gather(attended, "core", axis=0, tiled=True)
    terms = jnp.einsum(
        "tk,nk->tn", chip_att, w_share, preferred_element_type=jnp.float32
    ).astype(jnp.bfloat16)
    kvs = lax.axis_size("kv")
    per_c = terms.shape[1] // kvs
    routed = (
        terms.reshape(cores, tok_rows, kvs, per_c)
        .transpose(2, 0, 1, 3)
        .reshape(kvs * cores, tok_rows, per_c)
    )
    got = lax.all_to_all(routed, ("kv", "core"), 0, 0, tiled=True)
    total = jnp.sum(got.reshape(kvs, cores, tok_rows, per_c).astype(jnp.float32), axis=0)
    rows = out_weight.shape[0]
    hidden = (
        total.reshape(cores, tok_rows, per_c // rows, rows)
        .transpose(1, 2, 0, 3)
        .reshape(tok_rows, cores * per_c)
        .astype(jnp.bfloat16)
    )
    return (hidden, rot_keys)


def solution(mesh):
    kv_size, blk_size = mesh.devices.shape
    sub = Mesh(mesh.devices.reshape(kv_size, blk_size // 2, 2), ("kv",) + BLK)
    return jax.shard_map(
        body,
        mesh=sub,
        in_specs=(P(BLK, "kv"), P(BLK, "kv"), P(BLK, "kv"), P(), P(BLK, "kv")),
        out_specs=(P(BLK, "kv"), P(BLK, "kv")),
        check_vma=False,
    )
```

```python
import jax
import jax.numpy as jnp
import numpy as np
from jax import lax
from jax.sharding import Mesh
from jax.sharding import PartitionSpec as P

rope_base = 500000.0
BLK = ("chip", "core")


def locate(index, starts):
    hit = starts[None, :] <= index[:, None]
    segment = jnp.sum(hit.astype(jnp.int32), axis=1) - 1
    offset = jnp.max(jnp.where(hit, starts[None, :], 0), axis=1)
    return (segment, offset)


def half_swap(width, head_size):
    half = head_size // 2
    col = np.arange(width)
    within = col % head_size
    src = np.where(within < half, col + half, col - half)
    sign = np.where(within < half, -1.0, 1.0)
    swap = np.zeros((width, width), np.float32)
    swap[src, col] = sign
    return jnp.asarray(swap, jnp.bfloat16)


def rotate_flat(field, positions, head_size):
    half = head_size // 2
    steps = jnp.arange(half).astype(jnp.float32) * (2.0 / head_size)
    inverse = jnp.power(jnp.float32(rope_base), -steps)
    angle = positions.astype(jnp.float32)[:, None] * inverse[None, :]
    reps = field.shape[1] // head_size
    cosine = jnp.tile(jnp.cos(angle), (1, 2 * reps))
    sine = jnp.tile(jnp.sin(angle), (1, 2 * reps))
    swapped = jnp.dot(
        field, half_swap(field.shape[1], head_size), preferred_element_type=jnp.float32
    )
    return field.astype(jnp.float32) * cosine + swapped * sine


def body(queries, keys, values, lengths, out_weight):
    tok_rows = queries.shape[0]
    head_size = keys.shape[1]
    groups = queries.shape[1] // head_size
    cores = lax.axis_size("core")
    chips = lax.axis_size("chip")
    total_len = tok_rows * chips * cores
    seg_id = jnp.arange(lengths.shape[0] + 1)[:, None]
    short_id = jnp.arange(lengths.shape[0])[None, :]
    tail = jnp.sum(jnp.where(short_id >= seg_id - 1, lengths[None, :], 0), axis=1)
    starts = jnp.where(seg_id[:, 0] == 0, 0, total_len - tail)
    blk_idx = lax.axis_index("chip") * cores + lax.axis_index("core")
    first_tok = blk_idx * tok_rows
    query_idx = first_tok + jnp.arange(tok_rows)
    query_seg, query_off = locate(query_idx, starts)
    positions = query_idx - query_off
    if chips <= 8:
        held = [out_weight] + [
            lax.ppermute(out_weight, "chip", [(i, (i + s) % chips) for i in range(chips)])
            for s in range(1, chips)
        ]
        back = jnp.stack(held[::-1] + held[::-1], axis=0)
        here = lax.axis_index("chip")
        w_share = lax.dynamic_slice_in_dim(back, chips - 1 - here, chips, 0).reshape(
            chips * out_weight.shape[0], out_weight.shape[1]
        )
    else:
        w_share = lax.all_gather(out_weight, "chip", axis=0, tiled=True)
    rot_keys = rotate_flat(keys, positions, head_size).astype(jnp.bfloat16)
    rot_queries = rotate_flat(queries, positions, head_size).astype(jnp.bfloat16)
    query_rows = jnp.concatenate(
        [rot_queries[:, h * head_size:(h + 1) * head_size] for h in range(groups)], axis=0
    )
    row_idx = jnp.tile(query_idx, groups)
    row_seg = jnp.tile(query_seg, groups)
    scale = 1.0 / head_size**0.5
    kv_pair = lax.all_gather(
        jnp.concatenate([rot_keys, values], axis=1), BLK, axis=0, tiled=True
    )
    key_piece = kv_pair[:, :head_size]
    value_piece = kv_pair[:, head_size:]
    span = key_piece.shape[0]
    key_idx = jnp.arange(span)
    key_seg, key_off = locate(key_idx, starts)
    live = (key_seg[None, :] == row_seg[:, None]) & (key_idx[None, :] <= row_idx[:, None])
    scores = (
        jnp.einsum("rd,nd->rn", query_rows, key_piece, preferred_element_type=jnp.float32) * scale
    )
    scores = jnp.where(live, scores, -1e30)
    new_max = jnp.max(scores, axis=1)
    probs = jnp.where(live, jnp.exp(scores - new_max[:, None]), 0.0)
    new_sum = jnp.sum(probs, axis=1)
    new_weighted = jnp.dot(
        probs.astype(jnp.bfloat16), value_piece, preferred_element_type=jnp.float32
    )
    att_rows = (new_weighted / new_sum[:, None]).astype(jnp.bfloat16)
    attended = jnp.concatenate(
        [att_rows[h * tok_rows:(h + 1) * tok_rows] for h in range(groups)], axis=1
    )
    chip_att = lax.all_gather(attended, "core", axis=0, tiled=True)
    kvs = lax.axis_size("kv")
    per_c = w_share.shape[0] // kvs
    routed = jnp.stack(
        [
            jnp.dot(
                chip_att,
                w_share[c * per_c:(c + 1) * per_c].T,
                preferred_element_type=jnp.float32,
            ).astype(jnp.bfloat16)
            for c in range(kvs)
        ],
        axis=0,
    ).reshape(kvs * cores, tok_rows, per_c)
    got = lax.all_to_all(routed, ("kv", "core"), 0, 0, tiled=True)
    total = jnp.sum(got.reshape(kvs, cores, tok_rows, per_c).astype(jnp.float32), axis=0)
    rows = out_weight.shape[0]
    hidden = (
        total.reshape(cores, tok_rows, per_c // rows, rows)
        .transpose(1, 2, 0, 3)
        .reshape(tok_rows, cores * per_c)
        .astype(jnp.bfloat16)
    )
    return (hidden, rot_keys)


def solution(mesh):
    kv_size, blk_size = mesh.devices.shape
    sub = Mesh(mesh.devices.reshape(kv_size, blk_size // 2, 2), ("kv",) + BLK)
    return jax.shard_map(
        body,
        mesh=sub,
        in_specs=(P(BLK, "kv"), P(BLK, "kv"), P(BLK, "kv"), P(), P(BLK, "kv")),
        out_specs=(P(BLK, "kv"), P(BLK, "kv")),
        check_vma=False,
    )
```

```python
import jax
import jax.numpy as jnp
import numpy as np
from jax import lax
from jax.sharding import Mesh
from jax.sharding import PartitionSpec as P

rope_base = 500000.0
BLK = ("chip", "core")


def locate(index, starts):
    hit = starts[None, :] <= index[:, None]
    segment = jnp.sum(hit.astype(jnp.int32), axis=1) - 1
    offset = jnp.max(jnp.where(hit, starts[None, :], 0), axis=1)
    return (segment, offset)


def half_swap(width, head_size):
    half = head_size // 2
    col = np.arange(width)
    within = col % head_size
    src = np.where(within < half, col + half, col - half)
    sign = np.where(within < half, -1.0, 1.0)
    swap = np.zeros((width, width), np.float32)
    swap[src, col] = sign
    return jnp.asarray(swap, jnp.bfloat16)


def rotate_flat(field, positions, head_size):
    half = head_size // 2
    steps = jnp.arange(half).astype(jnp.float32) * (2.0 / head_size)
    inverse = jnp.power(jnp.float32(rope_base), -steps)
    angle = positions.astype(jnp.float32)[:, None] * inverse[None, :]
    reps = field.shape[1] // head_size
    cosine = jnp.tile(jnp.cos(angle), (1, 2 * reps))
    sine = jnp.tile(jnp.sin(angle), (1, 2 * reps))
    swapped = jnp.dot(
        field, half_swap(field.shape[1], head_size), preferred_element_type=jnp.float32
    )
    return field.astype(jnp.float32) * cosine + swapped * sine


def body(queries, keys, values, lengths, out_weight):
    tok_rows = queries.shape[0]
    head_size = keys.shape[1]
    groups = queries.shape[1] // head_size
    cores = lax.axis_size("core")
    chips = lax.axis_size("chip")
    total_len = tok_rows * chips * cores
    seg_id = jnp.arange(lengths.shape[0] + 1)[:, None]
    short_id = jnp.arange(lengths.shape[0])[None, :]
    tail = jnp.sum(jnp.where(short_id >= seg_id - 1, lengths[None, :], 0), axis=1)
    starts = jnp.where(seg_id[:, 0] == 0, 0, total_len - tail)
    blk_idx = lax.axis_index("chip") * cores + lax.axis_index("core")
    first_tok = blk_idx * tok_rows
    query_idx = first_tok + jnp.arange(tok_rows)
    query_seg, query_off = locate(query_idx, starts)
    positions = query_idx - query_off
    if chips <= 8:
        held = [out_weight] + [
            lax.ppermute(out_weight, "chip", [(i, (i + s) % chips) for i in range(chips)])
            for s in range(1, chips)
        ]
        back = jnp.stack(held[::-1] + held[::-1], axis=0)
        here = lax.axis_index("chip")
        w_share = lax.dynamic_slice_in_dim(back, chips - 1 - here, chips, 0).reshape(
            chips * out_weight.shape[0], out_weight.shape[1]
        )
    else:
        w_share = lax.all_gather(out_weight, "chip", axis=0, tiled=True)
    rot_keys = rotate_flat(keys, positions, head_size).astype(jnp.bfloat16)
    rot_queries = rotate_flat(queries, positions, head_size).astype(jnp.bfloat16)
    width = queries.shape[1]
    chip_rows = lax.all_gather(
        jnp.concatenate([rot_queries, rot_keys, values], axis=1), "core", axis=0, tiled=True
    )
    kv_pair = lax.all_gather(chip_rows[:, width:], "chip", axis=0, tiled=True)
    chip_q = chip_rows[:, :width]
    chip_tok = cores * tok_rows
    chip_idx = lax.axis_index("chip") * chip_tok + jnp.arange(chip_tok)
    chip_seg, _ = locate(chip_idx, starts)
    query_rows = jnp.concatenate(
        [chip_q[:, h * head_size:(h + 1) * head_size] for h in range(groups)], axis=0
    )
    row_idx = jnp.tile(chip_idx, groups)
    row_seg = jnp.tile(chip_seg, groups)
    scale = 1.0 / head_size**0.5
    key_piece = kv_pair[:, :head_size]
    value_piece = kv_pair[:, head_size:]
    span = key_piece.shape[0]
    key_idx = jnp.arange(span)
    key_seg, key_off = locate(key_idx, starts)
    live = (key_seg[None, :] == row_seg[:, None]) & (key_idx[None, :] <= row_idx[:, None])
    scores = (
        jnp.einsum("rd,nd->rn", query_rows, key_piece, preferred_element_type=jnp.float32) * scale
    )
    scores = jnp.where(live, scores, -1e30)
    new_max = jnp.max(scores, axis=1)
    probs = jnp.where(live, jnp.exp(scores - new_max[:, None]), 0.0)
    new_sum = jnp.sum(probs, axis=1)
    new_weighted = jnp.dot(
        probs.astype(jnp.bfloat16), value_piece, preferred_element_type=jnp.float32
    )
    att_rows = (new_weighted / new_sum[:, None]).astype(jnp.bfloat16)
    chip_att = jnp.concatenate(
        [att_rows[h * chip_tok:(h + 1) * chip_tok] for h in range(groups)], axis=1
    )
    kvs = lax.axis_size("kv")
    per_c = w_share.shape[0] // kvs
    routed = jnp.stack(
        [
            jnp.dot(
                chip_att,
                w_share[c * per_c:(c + 1) * per_c].T,
                preferred_element_type=jnp.float32,
            ).astype(jnp.bfloat16)
            for c in range(kvs)
        ],
        axis=0,
    ).reshape(kvs * cores, tok_rows, per_c)
    got = lax.all_to_all(routed, ("kv", "core"), 0, 0, tiled=True)
    total = jnp.sum(got.reshape(kvs, cores, tok_rows, per_c).astype(jnp.float32), axis=0)
    rows = out_weight.shape[0]
    hidden = (
        total.reshape(cores, tok_rows, per_c // rows, rows)
        .transpose(1, 2, 0, 3)
        .reshape(tok_rows, cores * per_c)
        .astype(jnp.bfloat16)
    )
    return (hidden, rot_keys)


def solution(mesh):
    kv_size, blk_size = mesh.devices.shape
    sub = Mesh(mesh.devices.reshape(kv_size, blk_size // 2, 2), ("kv",) + BLK)
    return jax.shard_map(
        body,
        mesh=sub,
        in_specs=(P(BLK, "kv"), P(BLK, "kv"), P(BLK, "kv"), P(), P(BLK, "kv")),
        out_specs=(P(BLK, "kv"), P(BLK, "kv")),
        check_vma=False,
    )
```

```python
import jax
import jax.numpy as jnp
import numpy as np
from jax import lax
from jax.sharding import Mesh
from jax.sharding import PartitionSpec as P

rope_base = 500000.0
BLK = ("chip", "core")


def locate(index, starts):
    hit = starts[None, :] <= index[:, None]
    segment = jnp.sum(hit.astype(jnp.int32), axis=1) - 1
    offset = jnp.max(jnp.where(hit, starts[None, :], 0), axis=1)
    return (segment, offset)


def half_swap(width, head_size):
    half = head_size // 2
    col = np.arange(width)
    within = col % head_size
    src = np.where(within < half, col + half, col - half)
    sign = np.where(within < half, -1.0, 1.0)
    swap = np.zeros((width, width), np.float32)
    swap[src, col] = sign
    return jnp.asarray(swap, jnp.bfloat16)


def rotate_flat(field, positions, head_size):
    half = head_size // 2
    steps = jnp.arange(half).astype(jnp.float32) * (2.0 / head_size)
    inverse = jnp.power(jnp.float32(rope_base), -steps)
    angle = positions.astype(jnp.float32)[:, None] * inverse[None, :]
    reps = field.shape[1] // head_size
    cosine = jnp.tile(jnp.cos(angle), (1, 2 * reps))
    sine = jnp.tile(jnp.sin(angle), (1, 2 * reps))
    swapped = jnp.dot(
        field, half_swap(field.shape[1], head_size), preferred_element_type=jnp.float32
    )
    return field.astype(jnp.float32) * cosine + swapped * sine


def body(queries, keys, values, lengths, out_weight):
    tok_rows = queries.shape[0]
    head_size = keys.shape[1]
    groups = queries.shape[1] // head_size
    cores = lax.axis_size("core")
    chips = lax.axis_size("chip")
    total_len = tok_rows * chips * cores
    seg_id = jnp.arange(lengths.shape[0] + 1)[:, None]
    short_id = jnp.arange(lengths.shape[0])[None, :]
    tail = jnp.sum(jnp.where(short_id >= seg_id - 1, lengths[None, :], 0), axis=1)
    starts = jnp.where(seg_id[:, 0] == 0, 0, total_len - tail)
    blk_idx = lax.axis_index("chip") * cores + lax.axis_index("core")
    first_tok = blk_idx * tok_rows
    query_idx = first_tok + jnp.arange(tok_rows)
    query_seg, query_off = locate(query_idx, starts)
    positions = query_idx - query_off
    rot_keys = rotate_flat(keys, positions, head_size).astype(jnp.bfloat16)
    rot_queries = rotate_flat(queries, positions, head_size).astype(jnp.bfloat16)
    width = queries.shape[1]
    chip_rows = lax.all_gather(
        jnp.concatenate([rot_queries, rot_keys, values], axis=1), "core", axis=0, tiled=True
    )
    kv_pair = lax.all_gather(chip_rows[:, width:], "chip", axis=0, tiled=True)
    if chips <= 8:
        out_weight, kv_pair = lax.optimization_barrier((out_weight, kv_pair))
        held = [out_weight] + [
            lax.ppermute(out_weight, "chip", [(i, (i + s) % chips) for i in range(chips)])
            for s in range(1, chips)
        ]
        back = jnp.stack(held[::-1] + held[::-1], axis=0)
        here = lax.axis_index("chip")
        w_share = lax.dynamic_slice_in_dim(back, chips - 1 - here, chips, 0).reshape(
            chips * out_weight.shape[0], out_weight.shape[1]
        )
    else:
        w_share = lax.all_gather(out_weight, "chip", axis=0, tiled=True)
    chip_q = chip_rows[:, :width]
    chip_tok = cores * tok_rows
    chip_idx = lax.axis_index("chip") * chip_tok + jnp.arange(chip_tok)
    chip_seg, _ = locate(chip_idx, starts)
    query_rows = jnp.concatenate(
        [chip_q[:, h * head_size:(h + 1) * head_size] for h in range(groups)], axis=0
    )
    row_idx = jnp.tile(chip_idx, groups)
    row_seg = jnp.tile(chip_seg, groups)
    scale = 1.0 / head_size**0.5
    key_piece = kv_pair[:, :head_size]
    value_piece = kv_pair[:, head_size:]
    span = key_piece.shape[0]
    key_idx = jnp.arange(span)
    key_seg, key_off = locate(key_idx, starts)
    live = (key_seg[None, :] == row_seg[:, None]) & (key_idx[None, :] <= row_idx[:, None])
    scores = (
        jnp.einsum("rd,nd->rn", query_rows, key_piece, preferred_element_type=jnp.float32) * scale
    )
    scores = jnp.where(live, scores, -1e30)
    new_max = jnp.max(scores, axis=1)
    probs = jnp.where(live, jnp.exp(scores - new_max[:, None]), 0.0)
    new_sum = jnp.sum(probs, axis=1)
    new_weighted = jnp.dot(
        probs.astype(jnp.bfloat16), value_piece, preferred_element_type=jnp.float32
    )
    att_rows = (new_weighted / new_sum[:, None]).astype(jnp.bfloat16)
    chip_att = jnp.concatenate(
        [att_rows[h * chip_tok:(h + 1) * chip_tok] for h in range(groups)], axis=1
    )
    kvs = lax.axis_size("kv")
    per_c = w_share.shape[0] // kvs
    routed = jnp.stack(
        [
            jnp.dot(
                chip_att,
                w_share[c * per_c:(c + 1) * per_c].T,
                preferred_element_type=jnp.float32,
            ).astype(jnp.bfloat16)
            for c in range(kvs)
        ],
        axis=0,
    ).reshape(kvs * cores, tok_rows, per_c)
    got = lax.all_to_all(routed, ("kv", "core"), 0, 0, tiled=True)
    total = jnp.sum(got.reshape(kvs, cores, tok_rows, per_c).astype(jnp.float32), axis=0)
    rows = out_weight.shape[0]
    hidden = (
        total.reshape(cores, tok_rows, per_c // rows, rows)
        .transpose(1, 2, 0, 3)
        .reshape(tok_rows, cores * per_c)
        .astype(jnp.bfloat16)
    )
    return (hidden, rot_keys)


def solution(mesh):
    kv_size, blk_size = mesh.devices.shape
    sub = Mesh(mesh.devices.reshape(kv_size, blk_size // 2, 2), ("kv",) + BLK)
    return jax.shard_map(
        body,
        mesh=sub,
        in_specs=(P(BLK, "kv"), P(BLK, "kv"), P(BLK, "kv"), P(), P(BLK, "kv")),
        out_specs=(P(BLK, "kv"), P(BLK, "kv")),
        check_vma=False,
    )
```

```python
import jax
import jax.numpy as jnp
import numpy as np
from jax import lax
from jax.sharding import Mesh
from jax.sharding import PartitionSpec as P

rope_base = 500000.0
BLK = ("chip", "core")


def locate(index, starts):
    hit = starts[None, :] <= index[:, None]
    segment = jnp.sum(hit.astype(jnp.int32), axis=1) - 1
    offset = jnp.max(jnp.where(hit, starts[None, :], 0), axis=1)
    return (segment, offset)


def half_swap(width, head_size):
    half = head_size // 2
    col = np.arange(width)
    within = col % head_size
    src = np.where(within < half, col + half, col - half)
    sign = np.where(within < half, -1.0, 1.0)
    swap = np.zeros((width, width), np.float32)
    swap[src, col] = sign
    return jnp.asarray(swap, jnp.bfloat16)


def rotate_flat(field, positions, head_size):
    half = head_size // 2
    steps = jnp.arange(half).astype(jnp.float32) * (2.0 / head_size)
    inverse = jnp.power(jnp.float32(rope_base), -steps)
    angle = positions.astype(jnp.float32)[:, None] * inverse[None, :]
    reps = field.shape[1] // head_size
    cosine = jnp.tile(jnp.cos(angle), (1, 2 * reps))
    sine = jnp.tile(jnp.sin(angle), (1, 2 * reps))
    swapped = jnp.dot(
        field, half_swap(field.shape[1], head_size), preferred_element_type=jnp.float32
    )
    return field.astype(jnp.float32) * cosine + swapped * sine


def gather_share(piece, chips):
    if chips > 8:
        return lax.all_gather(piece, "chip", axis=0, tiled=True)
    held = [piece] + [
        lax.ppermute(piece, "chip", [(i, (i + s) % chips) for i in range(chips)])
        for s in range(1, chips)
    ]
    back = jnp.stack(held[::-1] + held[::-1], axis=0)
    here = lax.axis_index("chip")
    return lax.dynamic_slice_in_dim(back, chips - 1 - here, chips, 0).reshape(
        chips * piece.shape[0], piece.shape[1]
    )


def project(chip_att, share, kvs, cores, tok_rows):
    per_c = share.shape[0] // kvs
    routed = jnp.stack(
        [
            jnp.dot(
                chip_att, share[c * per_c:(c + 1) * per_c].T, preferred_element_type=jnp.float32
            ).astype(jnp.bfloat16)
            for c in range(kvs)
        ],
        axis=0,
    ).reshape(kvs * cores, tok_rows, per_c)
    got = lax.all_to_all(routed, ("kv", "core"), 0, 0, tiled=True)
    return jnp.sum(got.reshape(kvs, cores, tok_rows, per_c).astype(jnp.float32), axis=0)


def body(queries, keys, values, lengths, out_weight):
    tok_rows = queries.shape[0]
    head_size = keys.shape[1]
    groups = queries.shape[1] // head_size
    cores = lax.axis_size("core")
    chips = lax.axis_size("chip")
    total_len = tok_rows * chips * cores
    seg_id = jnp.arange(lengths.shape[0] + 1)[:, None]
    short_id = jnp.arange(lengths.shape[0])[None, :]
    tail = jnp.sum(jnp.where(short_id >= seg_id - 1, lengths[None, :], 0), axis=1)
    starts = jnp.where(seg_id[:, 0] == 0, 0, total_len - tail)
    blk_idx = lax.axis_index("chip") * cores + lax.axis_index("core")
    first_tok = blk_idx * tok_rows
    query_idx = first_tok + jnp.arange(tok_rows)
    query_seg, query_off = locate(query_idx, starts)
    positions = query_idx - query_off
    rows = out_weight.shape[0]
    half_rows = rows // 2
    share_lo = gather_share(out_weight[:half_rows], chips)
    rot_keys = rotate_flat(keys, positions, head_size).astype(jnp.bfloat16)
    rot_queries = rotate_flat(queries, positions, head_size).astype(jnp.bfloat16)
    width = queries.shape[1]
    chip_rows = lax.all_gather(
        jnp.concatenate([rot_queries, rot_keys, values], axis=1), "core", axis=0, tiled=True
    )
    kv_pair = lax.all_gather(chip_rows[:, width:], "chip", axis=0, tiled=True)
    late_w, kv_pair = lax.optimization_barrier((out_weight[half_rows:], kv_pair))
    share_hi = gather_share(late_w, chips)
    chip_q = chip_rows[:, :width]
    chip_tok = cores * tok_rows
    chip_idx = lax.axis_index("chip") * chip_tok + jnp.arange(chip_tok)
    chip_seg, _ = locate(chip_idx, starts)
    query_rows = jnp.concatenate(
        [chip_q[:, h * head_size:(h + 1) * head_size] for h in range(groups)], axis=0
    )
    row_idx = jnp.tile(chip_idx, groups)
    row_seg = jnp.tile(chip_seg, groups)
    scale = 1.0 / head_size**0.5
    key_piece = kv_pair[:, :head_size]
    value_piece = kv_pair[:, head_size:]
    span = key_piece.shape[0]
    key_idx = jnp.arange(span)
    key_seg, key_off = locate(key_idx, starts)
    live = (key_seg[None, :] == row_seg[:, None]) & (key_idx[None, :] <= row_idx[:, None])
    scores = (
        jnp.einsum("rd,nd->rn", query_rows, key_piece, preferred_element_type=jnp.float32) * scale
    )
    scores = jnp.where(live, scores, -1e30)
    new_max = jnp.max(scores, axis=1)
    probs = jnp.where(live, jnp.exp(scores - new_max[:, None]), 0.0)
    new_sum = jnp.sum(probs, axis=1)
    new_weighted = jnp.dot(
        probs.astype(jnp.bfloat16), value_piece, preferred_element_type=jnp.float32
    )
    att_rows = (new_weighted / new_sum[:, None]).astype(jnp.bfloat16)
    chip_att = jnp.concatenate(
        [att_rows[h * chip_tok:(h + 1) * chip_tok] for h in range(groups)], axis=1
    )
    kvs = lax.axis_size("kv")
    parts = jnp.stack(
        [project(chip_att, share, kvs, cores, tok_rows) for share in (share_lo, share_hi)], 0
    )
    per_c = parts.shape[-1]
    hidden = (
        parts.reshape(2, cores, tok_rows, per_c // half_rows, half_rows)
        .transpose(2, 3, 1, 0, 4)
        .reshape(tok_rows, 2 * cores * per_c)
        .astype(jnp.bfloat16)
    )
    return (hidden, rot_keys)


def solution(mesh):
    kv_size, blk_size = mesh.devices.shape
    sub = Mesh(mesh.devices.reshape(kv_size, blk_size // 2, 2), ("kv",) + BLK)
    return jax.shard_map(
        body,
        mesh=sub,
        in_specs=(P(BLK, "kv"), P(BLK, "kv"), P(BLK, "kv"), P(), P(BLK, "kv")),
        out_specs=(P(BLK, "kv"), P(BLK, "kv")),
        check_vma=False,
    )
```

```python
import jax
import jax.numpy as jnp
import numpy as np
from jax import lax
from jax.sharding import Mesh
from jax.sharding import PartitionSpec as P

rope_base = 500000.0
BLK = ("chip", "core")


def locate(index, starts):
    hit = starts[None, :] <= index[:, None]
    segment = jnp.sum(hit.astype(jnp.int32), axis=1) - 1
    offset = jnp.max(jnp.where(hit, starts[None, :], 0), axis=1)
    return (segment, offset)


def half_swap(width, head_size):
    half = head_size // 2
    col = np.arange(width)
    within = col % head_size
    src = np.where(within < half, col + half, col - half)
    sign = np.where(within < half, -1.0, 1.0)
    swap = np.zeros((width, width), np.float32)
    swap[src, col] = sign
    return jnp.asarray(swap, jnp.bfloat16)


def rotate_flat(field, positions, head_size):
    half = head_size // 2
    steps = jnp.arange(half).astype(jnp.float32) * (2.0 / head_size)
    inverse = jnp.power(jnp.float32(rope_base), -steps)
    angle = positions.astype(jnp.float32)[:, None] * inverse[None, :]
    reps = field.shape[1] // head_size
    cosine = jnp.tile(jnp.cos(angle), (1, 2 * reps))
    sine = jnp.tile(jnp.sin(angle), (1, 2 * reps))
    swapped = jnp.dot(
        field, half_swap(field.shape[1], head_size), preferred_element_type=jnp.float32
    )
    return field.astype(jnp.float32) * cosine + swapped * sine


def body(queries, keys, values, lengths, out_weight):
    tok_rows = queries.shape[0]
    head_size = keys.shape[1]
    groups = queries.shape[1] // head_size
    cores = lax.axis_size("core")
    chips = lax.axis_size("chip")
    total_len = tok_rows * chips * cores
    seg_id = jnp.arange(lengths.shape[0] + 1)[:, None]
    short_id = jnp.arange(lengths.shape[0])[None, :]
    tail = jnp.sum(jnp.where(short_id >= seg_id - 1, lengths[None, :], 0), axis=1)
    starts = jnp.where(seg_id[:, 0] == 0, 0, total_len - tail)
    blk_idx = lax.axis_index("chip") * cores + lax.axis_index("core")
    first_tok = blk_idx * tok_rows
    query_idx = first_tok + jnp.arange(tok_rows)
    query_seg, query_off = locate(query_idx, starts)
    positions = query_idx - query_off
    if chips <= 8:
        held = [out_weight] + [
            lax.ppermute(out_weight, "chip", [(i, (i + s) % chips) for i in range(chips)])
            for s in range(1, chips)
        ]
        back = jnp.stack(held[::-1] + held[::-1], axis=0)
        here = lax.axis_index("chip")
        w_share = lax.dynamic_slice_in_dim(back, chips - 1 - here, chips, 0).reshape(
            chips * out_weight.shape[0], out_weight.shape[1]
        )
    else:
        w_share = lax.all_gather(out_weight, "chip", axis=0, tiled=True)
    rot_keys = rotate_flat(keys, positions, head_size).astype(jnp.bfloat16)
    rot_queries = rotate_flat(queries, positions, head_size).astype(jnp.bfloat16)
    width = queries.shape[1]
    chip_rows = lax.all_gather(
        jnp.concatenate([rot_queries, rot_keys, values], axis=1), "core", axis=0, tiled=True
    )
    chip_kv = chip_rows[:, width:]
    if chips <= 8:
        kv_pair = jnp.concatenate(
            [chip_kv]
            + [
                lax.ppermute(chip_kv, "chip", [(i, (i + s) % chips) for i in range(chips)])
                for s in range(1, chips)
            ],
            axis=0,
        )
        src_chip = (lax.axis_index("chip") - jnp.arange(chips)) % chips
    else:
        kv_pair = lax.all_gather(chip_kv, "chip", axis=0, tiled=True)
        src_chip = jnp.arange(chips)
    chip_q = chip_rows[:, :width]
    chip_tok = cores * tok_rows
    chip_idx = lax.axis_index("chip") * chip_tok + jnp.arange(chip_tok)
    chip_seg, _ = locate(chip_idx, starts)
    query_rows = jnp.concatenate(
        [chip_q[:, h * head_size:(h + 1) * head_size] for h in range(groups)], axis=0
    )
    row_idx = jnp.tile(chip_idx, groups)
    row_seg = jnp.tile(chip_seg, groups)
    scale = 1.0 / head_size**0.5
    key_piece = kv_pair[:, :head_size]
    value_piece = kv_pair[:, head_size:]
    span = key_piece.shape[0]
    chip_tok_kv = chip_kv.shape[0]
    key_idx = (src_chip[:, None] * chip_tok_kv + jnp.arange(chip_tok_kv)[None, :]).reshape(span)
    key_seg, key_off = locate(key_idx, starts)
    live = (key_seg[None, :] == row_seg[:, None]) & (key_idx[None, :] <= row_idx[:, None])
    scores = (
        jnp.einsum("rd,nd->rn", query_rows, key_piece, preferred_element_type=jnp.float32) * scale
    )
    scores = jnp.where(live, scores, -1e30)
    new_max = jnp.max(scores, axis=1)
    probs = jnp.where(live, jnp.exp(scores - new_max[:, None]), 0.0)
    new_sum = jnp.sum(probs, axis=1)
    new_weighted = jnp.dot(
        probs.astype(jnp.bfloat16), value_piece, preferred_element_type=jnp.float32
    )
    att_rows = (new_weighted / new_sum[:, None]).astype(jnp.bfloat16)
    chip_att = jnp.concatenate(
        [att_rows[h * chip_tok:(h + 1) * chip_tok] for h in range(groups)], axis=1
    )
    kvs = lax.axis_size("kv")
    per_c = w_share.shape[0] // kvs
    routed = jnp.stack(
        [
            jnp.dot(
                chip_att,
                w_share[c * per_c:(c + 1) * per_c].T,
                preferred_element_type=jnp.float32,
            ).astype(jnp.bfloat16)
            for c in range(kvs)
        ],
        axis=0,
    ).reshape(kvs * cores, tok_rows, per_c)
    got = lax.all_to_all(routed, ("kv", "core"), 0, 0, tiled=True)
    total = jnp.sum(got.reshape(kvs, cores, tok_rows, per_c).astype(jnp.float32), axis=0)
    rows = out_weight.shape[0]
    hidden = (
        total.reshape(cores, tok_rows, per_c // rows, rows)
        .transpose(1, 2, 0, 3)
        .reshape(tok_rows, cores * per_c)
        .astype(jnp.bfloat16)
    )
    return (hidden, rot_keys)


def solution(mesh):
    kv_size, blk_size = mesh.devices.shape
    sub = Mesh(mesh.devices.reshape(kv_size, blk_size // 2, 2), ("kv",) + BLK)
    return jax.shard_map(
        body,
        mesh=sub,
        in_specs=(P(BLK, "kv"), P(BLK, "kv"), P(BLK, "kv"), P(), P(BLK, "kv")),
        out_specs=(P(BLK, "kv"), P(BLK, "kv")),
        check_vma=False,
    )
```

```python
import jax
import jax.numpy as jnp
import numpy as np
from jax import lax
from jax.sharding import Mesh
from jax.sharding import PartitionSpec as P

rope_base = 500000.0
BLK = ("chip", "core")


def locate(index, starts):
    hit = starts[None, :] <= index[:, None]
    segment = jnp.sum(hit.astype(jnp.int32), axis=1) - 1
    offset = jnp.max(jnp.where(hit, starts[None, :], 0), axis=1)
    return (segment, offset)


def half_swap(width, head_size):
    half = head_size // 2
    col = np.arange(width)
    within = col % head_size
    src = np.where(within < half, col + half, col - half)
    sign = np.where(within < half, -1.0, 1.0)
    swap = np.zeros((width, width), np.float32)
    swap[src, col] = sign
    return jnp.asarray(swap, jnp.bfloat16)


def rotate_flat(field, positions, head_size):
    half = head_size // 2
    steps = jnp.arange(half).astype(jnp.float32) * (2.0 / head_size)
    inverse = jnp.power(jnp.float32(rope_base), -steps)
    angle = positions.astype(jnp.float32)[:, None] * inverse[None, :]
    reps = field.shape[1] // head_size
    cosine = jnp.tile(jnp.cos(angle), (1, 2 * reps))
    sine = jnp.tile(jnp.sin(angle), (1, 2 * reps))
    swapped = jnp.dot(
        field, half_swap(field.shape[1], head_size), preferred_element_type=jnp.float32
    )
    return field.astype(jnp.float32) * cosine + swapped * sine


def body(queries, keys, values, lengths, out_weight):
    tok_rows = queries.shape[0]
    head_size = keys.shape[1]
    groups = queries.shape[1] // head_size
    cores = lax.axis_size("core")
    chips = lax.axis_size("chip")
    total_len = tok_rows * chips * cores
    seg_id = jnp.arange(lengths.shape[0] + 1)[:, None]
    short_id = jnp.arange(lengths.shape[0])[None, :]
    tail = jnp.sum(jnp.where(short_id >= seg_id - 1, lengths[None, :], 0), axis=1)
    starts = jnp.where(seg_id[:, 0] == 0, 0, total_len - tail)
    blk_idx = lax.axis_index("chip") * cores + lax.axis_index("core")
    first_tok = blk_idx * tok_rows
    query_idx = first_tok + jnp.arange(tok_rows)
    query_seg, query_off = locate(query_idx, starts)
    positions = query_idx - query_off
    rot_keys = rotate_flat(keys, positions, head_size).astype(jnp.bfloat16)
    width = queries.shape[1]
    chip_rows = lax.all_gather(
        jnp.concatenate([queries, keys, values], axis=1), "core", axis=0, tiled=True
    )
    chip_kv = chip_rows[:, width:]
    out_weight, chip_kv = lax.optimization_barrier((out_weight, chip_kv))
    if chips <= 8:
        kv_pair = jnp.concatenate(
            [chip_kv]
            + [
                lax.ppermute(chip_kv, "chip", [(i, (i + s) % chips) for i in range(chips)])
                for s in range(1, chips)
            ],
            axis=0,
        )
        src_chip = (lax.axis_index("chip") - jnp.arange(chips)) % chips
    else:
        kv_pair = lax.all_gather(chip_kv, "chip", axis=0, tiled=True)
        src_chip = jnp.arange(chips)
    if chips <= 8:
        held = [out_weight] + [
            lax.ppermute(out_weight, "chip", [(i, (i + s) % chips) for i in range(chips)])
            for s in range(1, chips)
        ]
        back = jnp.stack(held[::-1] + held[::-1], axis=0)
        here = lax.axis_index("chip")
        w_share = lax.dynamic_slice_in_dim(back, chips - 1 - here, chips, 0).reshape(
            chips * out_weight.shape[0], out_weight.shape[1]
        )
    else:
        w_share = lax.all_gather(out_weight, "chip", axis=0, tiled=True)
    chip_q = chip_rows[:, :width]
    chip_tok = cores * tok_rows
    chip_idx = lax.axis_index("chip") * chip_tok + jnp.arange(chip_tok)
    chip_seg, chip_off = locate(chip_idx, starts)
    chip_q = rotate_flat(chip_q, chip_idx - chip_off, head_size).astype(jnp.bfloat16)
    query_rows = jnp.concatenate(
        [chip_q[:, h * head_size:(h + 1) * head_size] for h in range(groups)], axis=0
    )
    row_idx = jnp.tile(chip_idx, groups)
    row_seg = jnp.tile(chip_seg, groups)
    scale = 1.0 / head_size**0.5
    value_piece = kv_pair[:, head_size:]
    span = kv_pair.shape[0]
    chip_tok_kv = chip_kv.shape[0]
    key_idx = (src_chip[:, None] * chip_tok_kv + jnp.arange(chip_tok_kv)[None, :]).reshape(span)
    key_seg, key_off = locate(key_idx, starts)
    key_piece = rotate_flat(kv_pair[:, :head_size], key_idx - key_off, head_size).astype(
        jnp.bfloat16
    )
    live = (key_seg[None, :] == row_seg[:, None]) & (key_idx[None, :] <= row_idx[:, None])
    scores = (
        jnp.einsum("rd,nd->rn", query_rows, key_piece, preferred_element_type=jnp.float32) * scale
    )
    scores = jnp.where(live, scores, -1e30)
    new_max = jnp.max(scores, axis=1)
    probs = jnp.where(live, jnp.exp(scores - new_max[:, None]), 0.0)
    new_sum = jnp.sum(probs, axis=1)
    new_weighted = jnp.dot(
        probs.astype(jnp.bfloat16), value_piece, preferred_element_type=jnp.float32
    )
    att_rows = (new_weighted / new_sum[:, None]).astype(jnp.bfloat16)
    chip_att = jnp.concatenate(
        [att_rows[h * chip_tok:(h + 1) * chip_tok] for h in range(groups)], axis=1
    )
    kvs = lax.axis_size("kv")
    per_c = w_share.shape[0] // kvs
    routed = jnp.stack(
        [
            jnp.dot(
                chip_att,
                w_share[c * per_c:(c + 1) * per_c].T,
                preferred_element_type=jnp.float32,
            ).astype(jnp.bfloat16)
            for c in range(kvs)
        ],
        axis=0,
    ).reshape(kvs * cores, tok_rows, per_c)
    got = lax.all_to_all(routed, ("kv", "core"), 0, 0, tiled=True)
    total = jnp.sum(got.reshape(kvs, cores, tok_rows, per_c).astype(jnp.float32), axis=0)
    rows = out_weight.shape[0]
    hidden = (
        total.reshape(cores, tok_rows, per_c // rows, rows)
        .transpose(1, 2, 0, 3)
        .reshape(tok_rows, cores * per_c)
        .astype(jnp.bfloat16)
    )
    return (hidden, rot_keys)


def solution(mesh):
    kv_size, blk_size = mesh.devices.shape
    sub = Mesh(mesh.devices.reshape(kv_size, blk_size // 2, 2), ("kv",) + BLK)
    return jax.shard_map(
        body,
        mesh=sub,
        in_specs=(P(BLK, "kv"), P(BLK, "kv"), P(BLK, "kv"), P(), P(BLK, "kv")),
        out_specs=(P(BLK, "kv"), P(BLK, "kv")),
        check_vma=False,
    )
```

```python
import jax
import jax.numpy as jnp
import numpy as np
from jax import lax
from jax.sharding import Mesh
from jax.sharding import PartitionSpec as P

rope_base = 500000.0
BLK = ("chip", "core")


def locate(index, starts):
    hit = starts[None, :] <= index[:, None]
    segment = jnp.sum(hit.astype(jnp.int32), axis=1) - 1
    offset = jnp.max(jnp.where(hit, starts[None, :], 0), axis=1)
    return (segment, offset)


def half_swap(width, head_size):
    half = head_size // 2
    col = np.arange(width)
    within = col % head_size
    src = np.where(within < half, col + half, col - half)
    sign = np.where(within < half, -1.0, 1.0)
    swap = np.zeros((width, width), np.float32)
    swap[src, col] = sign
    return jnp.asarray(swap, jnp.bfloat16)


def rotate_flat(field, positions, head_size):
    half = head_size // 2
    steps = jnp.arange(half).astype(jnp.float32) * (2.0 / head_size)
    inverse = jnp.power(jnp.float32(rope_base), -steps)
    angle = positions.astype(jnp.float32)[:, None] * inverse[None, :]
    reps = field.shape[1] // head_size
    cosine = jnp.tile(jnp.cos(angle), (1, 2 * reps))
    sine = jnp.tile(jnp.sin(angle), (1, 2 * reps))
    swapped = jnp.dot(
        field, half_swap(field.shape[1], head_size), preferred_element_type=jnp.float32
    )
    return field.astype(jnp.float32) * cosine + swapped * sine


def body(queries, keys, values, lengths, out_weight):
    tok_rows = queries.shape[0]
    head_size = keys.shape[1]
    groups = queries.shape[1] // head_size
    cores = lax.axis_size("core")
    chips = lax.axis_size("chip")
    total_len = tok_rows * chips * cores
    seg_id = jnp.arange(lengths.shape[0] + 1)[:, None]
    short_id = jnp.arange(lengths.shape[0])[None, :]
    tail = jnp.sum(jnp.where(short_id >= seg_id - 1, lengths[None, :], 0), axis=1)
    starts = jnp.where(seg_id[:, 0] == 0, 0, total_len - tail)
    blk_idx = lax.axis_index("chip") * cores + lax.axis_index("core")
    first_tok = blk_idx * tok_rows
    query_idx = first_tok + jnp.arange(tok_rows)
    query_seg, query_off = locate(query_idx, starts)
    positions = query_idx - query_off
    rot_keys = rotate_flat(keys, positions, head_size).astype(jnp.bfloat16)
    width = queries.shape[1]
    chip_rows = lax.all_gather(
        jnp.concatenate([queries, keys, values], axis=1), "core", axis=0, tiled=True
    )
    chip_kv = chip_rows[:, width:]
    out_weight, chip_kv = lax.optimization_barrier((out_weight, chip_kv))
    if chips <= 8:
        ring = lambda s: [(i, (i + s) % chips) for i in range(chips)]
        kv_own = sorted({1, chips - 1} - {0})
        kv_held = {0: chip_kv}
        for s in kv_own:
            kv_held[s] = lax.ppermute(chip_kv, "chip", ring(s))
        kv_size = chip_kv.size
        held = [out_weight]
        for s in range(1, chips):
            if s in kv_held:
                held.append(lax.ppermute(out_weight, "chip", ring(s)))
            else:
                both = lax.ppermute(
                    jnp.concatenate([chip_kv.reshape(-1), out_weight.reshape(-1)]), "chip", ring(s)
                )
                kv_held[s] = both[:kv_size].reshape(chip_kv.shape)
                held.append(both[kv_size:].reshape(out_weight.shape))
        kv_pair = jnp.concatenate([kv_held[s] for s in range(chips)], axis=0)
        src_chip = (lax.axis_index("chip") - jnp.arange(chips)) % chips
        back = jnp.stack(held[::-1] + held[::-1], axis=0)
        here = lax.axis_index("chip")
        w_share = lax.dynamic_slice_in_dim(back, chips - 1 - here, chips, 0).reshape(
            chips * out_weight.shape[0], out_weight.shape[1]
        )
    else:
        kv_pair = lax.all_gather(chip_kv, "chip", axis=0, tiled=True)
        src_chip = jnp.arange(chips)
        w_share = lax.all_gather(out_weight, "chip", axis=0, tiled=True)
    chip_q = chip_rows[:, :width]
    chip_tok = cores * tok_rows
    chip_idx = lax.axis_index("chip") * chip_tok + jnp.arange(chip_tok)
    chip_seg, chip_off = locate(chip_idx, starts)
    chip_q = rotate_flat(chip_q, chip_idx - chip_off, head_size).astype(jnp.bfloat16)
    query_rows = jnp.concatenate(
        [chip_q[:, h * head_size:(h + 1) * head_size] for h in range(groups)], axis=0
    )
    row_idx = jnp.tile(chip_idx, groups)
    row_seg = jnp.tile(chip_seg, groups)
    scale = 1.0 / head_size**0.5
    value_piece = kv_pair[:, head_size:]
    span = kv_pair.shape[0]
    chip_tok_kv = chip_kv.shape[0]
    key_idx = (src_chip[:, None] * chip_tok_kv + jnp.arange(chip_tok_kv)[None, :]).reshape(span)
    key_seg, key_off = locate(key_idx, starts)
    key_piece = rotate_flat(kv_pair[:, :head_size], key_idx - key_off, head_size).astype(
        jnp.bfloat16
    )
    key_piece, value_piece = lax.optimization_barrier((key_piece, value_piece))
    live = (key_seg[None, :] == row_seg[:, None]) & (key_idx[None, :] <= row_idx[:, None])
    scores = (
        jnp.einsum("rd,nd->rn", query_rows, key_piece, preferred_element_type=jnp.float32) * scale
    )
    scores = jnp.where(live, scores, -1e30)
    new_max = jnp.max(scores, axis=1)
    probs = jnp.where(live, jnp.exp(scores - new_max[:, None]), 0.0)
    new_sum = jnp.sum(probs, axis=1)
    new_weighted = jnp.dot(
        probs.astype(jnp.bfloat16), value_piece, preferred_element_type=jnp.float32
    )
    att_rows = (new_weighted / new_sum[:, None]).astype(jnp.bfloat16)
    chip_att = jnp.concatenate(
        [att_rows[h * chip_tok:(h + 1) * chip_tok] for h in range(groups)], axis=1
    )
    kvs = lax.axis_size("kv")
    per_c = w_share.shape[0] // kvs
    routed = jnp.stack(
        [
            jnp.dot(
                chip_att,
                w_share[c * per_c:(c + 1) * per_c].T,
                preferred_element_type=jnp.float32,
            ).astype(jnp.bfloat16)
            for c in range(kvs)
        ],
        axis=0,
    ).reshape(kvs * cores, tok_rows, per_c)
    got = lax.all_to_all(routed, ("kv", "core"), 0, 0, tiled=True)
    total = jnp.sum(got.reshape(kvs, cores, tok_rows, per_c).astype(jnp.float32), axis=0)
    rows = out_weight.shape[0]
    hidden = (
        total.reshape(cores, tok_rows, per_c // rows, rows)
        .transpose(1, 2, 0, 3)
        .reshape(tok_rows, cores * per_c)
        .astype(jnp.bfloat16)
    )
    return (hidden, rot_keys)


def solution(mesh):
    kv_size, blk_size = mesh.devices.shape
    sub = Mesh(mesh.devices.reshape(kv_size, blk_size // 2, 2), ("kv",) + BLK)
    return jax.shard_map(
        body,
        mesh=sub,
        in_specs=(P(BLK, "kv"), P(BLK, "kv"), P(BLK, "kv"), P(), P(BLK, "kv")),
        out_specs=(P(BLK, "kv"), P(BLK, "kv")),
        check_vma=False,
    )
```

```python
import jax
import jax.numpy as jnp
import numpy as np
from jax import lax
from jax.sharding import Mesh
from jax.sharding import PartitionSpec as P

rope_base = 500000.0
BLK = ("chip", "core")


def locate(index, starts):
    hit = starts[None, :] <= index[:, None]
    segment = jnp.sum(hit.astype(jnp.int32), axis=1) - 1
    offset = jnp.max(jnp.where(hit, starts[None, :], 0), axis=1)
    return (segment, offset)


def half_swap(width, head_size):
    half = head_size // 2
    col = np.arange(width)
    within = col % head_size
    src = np.where(within < half, col + half, col - half)
    sign = np.where(within < half, -1.0, 1.0)
    swap = np.zeros((width, width), np.float32)
    swap[src, col] = sign
    return jnp.asarray(swap, jnp.bfloat16)


def rotate_flat(field, positions, head_size):
    half = head_size // 2
    steps = jnp.arange(half).astype(jnp.float32) * (2.0 / head_size)
    inverse = jnp.power(jnp.float32(rope_base), -steps)
    angle = positions.astype(jnp.float32)[:, None] * inverse[None, :]
    reps = field.shape[1] // head_size
    cosine = jnp.tile(jnp.cos(angle), (1, 2 * reps))
    sine = jnp.tile(jnp.sin(angle), (1, 2 * reps))
    swapped = jnp.dot(
        field, half_swap(field.shape[1], head_size), preferred_element_type=jnp.float32
    )
    return field.astype(jnp.float32) * cosine + swapped * sine


def body(queries, keys, values, lengths, out_weight):
    tok_rows = queries.shape[0]
    head_size = keys.shape[1]
    groups = queries.shape[1] // head_size
    cores = lax.axis_size("core")
    chips = lax.axis_size("chip")
    total_len = tok_rows * chips * cores
    seg_id = jnp.arange(lengths.shape[0] + 1)[:, None]
    short_id = jnp.arange(lengths.shape[0])[None, :]
    tail = jnp.sum(jnp.where(short_id >= seg_id - 1, lengths[None, :], 0), axis=1)
    starts = jnp.where(seg_id[:, 0] == 0, 0, total_len - tail)
    blk_idx = lax.axis_index("chip") * cores + lax.axis_index("core")
    first_tok = blk_idx * tok_rows
    query_idx = first_tok + jnp.arange(tok_rows)
    query_seg, query_off = locate(query_idx, starts)
    positions = query_idx - query_off
    if chips <= 8 and chips & (chips - 1) == 0:
        held = [out_weight] + [
            lax.ppermute(out_weight, "chip", [(i, i ^ d) for i in range(chips)])
            for d in range(1, chips)
        ]
        order = lax.axis_index("chip") ^ jnp.arange(chips)
        w_share = jnp.stack(held, axis=0)[order].reshape(
            chips * out_weight.shape[0], out_weight.shape[1]
        )
    else:
        w_share = lax.all_gather(out_weight, "chip", axis=0, tiled=True)
    rot_keys = rotate_flat(keys, positions, head_size).astype(jnp.bfloat16)
    rot_queries = rotate_flat(queries, positions, head_size).astype(jnp.bfloat16)
    width = queries.shape[1]
    chip_rows = lax.all_gather(
        jnp.concatenate([rot_queries, rot_keys, values], axis=1), "core", axis=0, tiled=True
    )
    chip_kv = chip_rows[:, width:]
    if chips <= 8 and chips & (chips - 1) == 0:
        kv_pair = jnp.concatenate(
            [chip_kv]
            + [
                lax.ppermute(chip_kv, "chip", [(i, i ^ d) for i in range(chips)])
                for d in range(1, chips)
            ],
            axis=0,
        )
        src_chip = lax.axis_index("chip") ^ jnp.arange(chips)
    else:
        kv_pair = lax.all_gather(chip_kv, "chip", axis=0, tiled=True)
        src_chip = jnp.arange(chips)
    chip_q = chip_rows[:, :width]
    chip_tok = cores * tok_rows
    chip_idx = lax.axis_index("chip") * chip_tok + jnp.arange(chip_tok)
    chip_seg, _ = locate(chip_idx, starts)
    query_rows = jnp.concatenate(
        [chip_q[:, h * head_size:(h + 1) * head_size] for h in range(groups)], axis=0
    )
    row_idx = jnp.tile(chip_idx, groups)
    row_seg = jnp.tile(chip_seg, groups)
    scale = 1.0 / head_size**0.5
    key_piece = kv_pair[:, :head_size]
    value_piece = kv_pair[:, head_size:]
    span = key_piece.shape[0]
    chip_tok_kv = chip_kv.shape[0]
    key_idx = (src_chip[:, None] * chip_tok_kv + jnp.arange(chip_tok_kv)[None, :]).reshape(span)
    key_seg, key_off = locate(key_idx, starts)
    live = (key_seg[None, :] == row_seg[:, None]) & (key_idx[None, :] <= row_idx[:, None])
    scores = (
        jnp.einsum("rd,nd->rn", query_rows, key_piece, preferred_element_type=jnp.float32) * scale
    )
    scores = jnp.where(live, scores, -1e30)
    new_max = jnp.max(scores, axis=1)
    probs = jnp.where(live, jnp.exp(scores - new_max[:, None]), 0.0)
    new_sum = jnp.sum(probs, axis=1)
    new_weighted = jnp.dot(
        probs.astype(jnp.bfloat16), value_piece, preferred_element_type=jnp.float32
    )
    att_rows = (new_weighted / new_sum[:, None]).astype(jnp.bfloat16)
    chip_att = jnp.concatenate(
        [att_rows[h * chip_tok:(h + 1) * chip_tok] for h in range(groups)], axis=1
    )
    kvs = lax.axis_size("kv")
    per_c = w_share.shape[0] // kvs
    routed = jnp.stack(
        [
            jnp.dot(
                chip_att,
                w_share[c * per_c:(c + 1) * per_c].T,
                preferred_element_type=jnp.float32,
            ).astype(jnp.bfloat16)
            for c in range(kvs)
        ],
        axis=0,
    ).reshape(kvs * cores, tok_rows, per_c)
    got = lax.all_to_all(routed, ("kv", "core"), 0, 0, tiled=True)
    total = jnp.sum(got.reshape(kvs, cores, tok_rows, per_c).astype(jnp.float32), axis=0)
    rows = out_weight.shape[0]
    hidden = (
        total.reshape(cores, tok_rows, per_c // rows, rows)
        .transpose(1, 2, 0, 3)
        .reshape(tok_rows, cores * per_c)
        .astype(jnp.bfloat16)
    )
    return (hidden, rot_keys)


def solution(mesh):
    kv_size, blk_size = mesh.devices.shape
    sub = Mesh(mesh.devices.reshape(kv_size, blk_size // 2, 2), ("kv",) + BLK)
    return jax.shard_map(
        body,
        mesh=sub,
        in_specs=(P(BLK, "kv"), P(BLK, "kv"), P(BLK, "kv"), P(), P(BLK, "kv")),
        out_specs=(P(BLK, "kv"), P(BLK, "kv")),
        check_vma=False,
    )
```

```python
import jax
import jax.numpy as jnp
import numpy as np
from jax import lax
from jax.sharding import Mesh
from jax.sharding import PartitionSpec as P

rope_base = 500000.0
BLK = ("chip", "core")


def locate(index, starts):
    hit = starts[None, :] <= index[:, None]
    segment = jnp.sum(hit.astype(jnp.int32), axis=1) - 1
    offset = jnp.max(jnp.where(hit, starts[None, :], 0), axis=1)
    return (segment, offset)


def half_swap(width, head_size):
    half = head_size // 2
    col = np.arange(width)
    within = col % head_size
    src = np.where(within < half, col + half, col - half)
    sign = np.where(within < half, -1.0, 1.0)
    swap = np.zeros((width, width), np.float32)
    swap[src, col] = sign
    return jnp.asarray(swap, jnp.bfloat16)


def rotate_flat(field, positions, head_size):
    half = head_size // 2
    steps = jnp.arange(half).astype(jnp.float32) * (2.0 / head_size)
    inverse = jnp.power(jnp.float32(rope_base), -steps)
    angle = positions.astype(jnp.float32)[:, None] * inverse[None, :]
    reps = field.shape[1] // head_size
    cosine = jnp.tile(jnp.cos(angle), (1, 2 * reps))
    sine = jnp.tile(jnp.sin(angle), (1, 2 * reps))
    swapped = jnp.dot(
        field, half_swap(field.shape[1], head_size), preferred_element_type=jnp.float32
    )
    return field.astype(jnp.float32) * cosine + swapped * sine


def body(queries, keys, values, lengths, out_weight):
    tok_rows = queries.shape[0]
    head_size = keys.shape[1]
    groups = queries.shape[1] // head_size
    cores = lax.axis_size("core")
    chips = lax.axis_size("chip")
    total_len = tok_rows * chips * cores
    seg_id = jnp.arange(lengths.shape[0] + 1)[:, None]
    short_id = jnp.arange(lengths.shape[0])[None, :]
    tail = jnp.sum(jnp.where(short_id >= seg_id - 1, lengths[None, :], 0), axis=1)
    starts = jnp.where(seg_id[:, 0] == 0, 0, total_len - tail)
    blk_idx = lax.axis_index("chip") * cores + lax.axis_index("core")
    first_tok = blk_idx * tok_rows
    query_idx = first_tok + jnp.arange(tok_rows)
    query_seg, query_off = locate(query_idx, starts)
    positions = query_idx - query_off
    rot_keys = rotate_flat(keys, positions, head_size).astype(jnp.bfloat16)
    width = queries.shape[1]
    chip_rows = lax.all_gather(
        jnp.concatenate([queries, keys, values], axis=1), "core", axis=0, tiled=True
    )
    chip_kv = chip_rows[:, width:]
    out_weight, chip_kv = lax.optimization_barrier((out_weight, chip_kv))
    if chips <= 8:
        kv_pair = jnp.concatenate(
            [chip_kv]
            + [
                lax.ppermute(chip_kv, "chip", [(i, (i + s) % chips) for i in range(chips)])
                for s in range(1, chips)
            ],
            axis=0,
        )
        src_chip = (lax.axis_index("chip") - jnp.arange(chips)) % chips
    else:
        kv_pair = lax.all_gather(chip_kv, "chip", axis=0, tiled=True)
        src_chip = jnp.arange(chips)
    if chips <= 8:
        held = [out_weight] + [
            lax.ppermute(out_weight, "chip", [(i, (i + s) % chips) for i in range(chips)])
            for s in range(1, chips)
        ]
        back = jnp.stack(held[::-1] + held[::-1], axis=0)
        here = lax.axis_index("chip")
        w_share = lax.dynamic_slice_in_dim(back, chips - 1 - here, chips, 0).reshape(
            chips * out_weight.shape[0], out_weight.shape[1]
        )
    else:
        w_share = lax.all_gather(out_weight, "chip", axis=0, tiled=True)
    kv_pair, chip_q = lax.optimization_barrier((kv_pair, chip_rows[:, :width]))
    chip_tok = cores * tok_rows
    chip_idx = lax.axis_index("chip") * chip_tok + jnp.arange(chip_tok)
    chip_seg, chip_off = locate(chip_idx, starts)
    chip_q = rotate_flat(chip_q, chip_idx - chip_off, head_size).astype(jnp.bfloat16)
    query_rows = jnp.concatenate(
        [chip_q[:, h * head_size:(h + 1) * head_size] for h in range(groups)], axis=0
    )
    row_idx = jnp.tile(chip_idx, groups)
    row_seg = jnp.tile(chip_seg, groups)
    scale = 1.0 / head_size**0.5
    value_piece = kv_pair[:, head_size:]
    span = kv_pair.shape[0]
    chip_tok_kv = chip_kv.shape[0]
    key_idx = (src_chip[:, None] * chip_tok_kv + jnp.arange(chip_tok_kv)[None, :]).reshape(span)
    key_seg, key_off = locate(key_idx, starts)
    key_piece = rotate_flat(kv_pair[:, :head_size], key_idx - key_off, head_size).astype(
        jnp.bfloat16
    )
    key_piece, value_piece = lax.optimization_barrier((key_piece, value_piece))
    live = (key_seg[None, :] == row_seg[:, None]) & (key_idx[None, :] <= row_idx[:, None])
    scores = (
        jnp.einsum("rd,nd->rn", query_rows, key_piece, preferred_element_type=jnp.float32) * scale
    )
    scores = jnp.where(live, scores, -1e30)
    new_max = jnp.max(scores, axis=1)
    probs = jnp.where(live, jnp.exp(scores - new_max[:, None]), 0.0)
    new_sum = jnp.sum(probs, axis=1)
    new_weighted = jnp.dot(
        probs.astype(jnp.bfloat16), value_piece, preferred_element_type=jnp.float32
    )
    att_rows = (new_weighted / new_sum[:, None]).astype(jnp.bfloat16)
    chip_att = jnp.concatenate(
        [att_rows[h * chip_tok:(h + 1) * chip_tok] for h in range(groups)], axis=1
    )
    kvs = lax.axis_size("kv")
    per_c = w_share.shape[0] // kvs
    routed = jnp.stack(
        [
            jnp.dot(
                chip_att,
                w_share[c * per_c:(c + 1) * per_c].T,
                preferred_element_type=jnp.float32,
            ).astype(jnp.bfloat16)
            for c in range(kvs)
        ],
        axis=0,
    ).reshape(kvs * cores, tok_rows, per_c)
    got = lax.all_to_all(routed, ("kv", "core"), 0, 0, tiled=True)
    total = jnp.sum(got.reshape(kvs, cores, tok_rows, per_c).astype(jnp.float32), axis=0)
    rows = out_weight.shape[0]
    hidden = (
        total.reshape(cores, tok_rows, per_c // rows, rows)
        .transpose(1, 2, 0, 3)
        .reshape(tok_rows, cores * per_c)
        .astype(jnp.bfloat16)
    )
    return (hidden, rot_keys)


def solution(mesh):
    kv_size, blk_size = mesh.devices.shape
    sub = Mesh(mesh.devices.reshape(kv_size, blk_size // 2, 2), ("kv",) + BLK)
    return jax.shard_map(
        body,
        mesh=sub,
        in_specs=(P(BLK, "kv"), P(BLK, "kv"), P(BLK, "kv"), P(), P(BLK, "kv")),
        out_specs=(P(BLK, "kv"), P(BLK, "kv")),
        check_vma=False,
    )
```

```python
import jax
import jax.numpy as jnp
import numpy as np
from jax import lax
from jax.sharding import Mesh
from jax.sharding import PartitionSpec as P

rope_base = 500000.0
BLK = ("chip", "core")


def locate(index, starts):
    hit = starts[None, :] <= index[:, None]
    segment = jnp.sum(hit.astype(jnp.int32), axis=1) - 1
    offset = jnp.max(jnp.where(hit, starts[None, :], 0), axis=1)
    return (segment, offset)


def half_swap(width, head_size):
    half = head_size // 2
    col = np.arange(width)
    within = col % head_size
    src = np.where(within < half, col + half, col - half)
    sign = np.where(within < half, -1.0, 1.0)
    swap = np.zeros((width, width), np.float32)
    swap[src, col] = sign
    return jnp.asarray(swap, jnp.bfloat16)


def rotate_flat(field, positions, head_size):
    half = head_size // 2
    steps = jnp.arange(half).astype(jnp.float32) * (2.0 / head_size)
    inverse = jnp.power(jnp.float32(rope_base), -steps)
    angle = positions.astype(jnp.float32)[:, None] * inverse[None, :]
    reps = field.shape[1] // head_size
    cosine = jnp.tile(jnp.cos(angle), (1, 2 * reps))
    sine = jnp.tile(jnp.sin(angle), (1, 2 * reps))
    swapped = jnp.dot(
        field, half_swap(field.shape[1], head_size), preferred_element_type=jnp.float32
    )
    return field.astype(jnp.float32) * cosine + swapped * sine


def body(queries, keys, values, lengths, out_weight):
    tok_rows = queries.shape[0]
    head_size = keys.shape[1]
    groups = queries.shape[1] // head_size
    cores = lax.axis_size("core")
    chips = lax.axis_size("chip")
    total_len = tok_rows * chips * cores
    seg_id = jnp.arange(lengths.shape[0] + 1)[:, None]
    short_id = jnp.arange(lengths.shape[0])[None, :]
    tail = jnp.sum(jnp.where(short_id >= seg_id - 1, lengths[None, :], 0), axis=1)
    starts = jnp.where(seg_id[:, 0] == 0, 0, total_len - tail)
    blk_idx = lax.axis_index("chip") * cores + lax.axis_index("core")
    first_tok = blk_idx * tok_rows
    query_idx = first_tok + jnp.arange(tok_rows)
    query_seg, query_off = locate(query_idx, starts)
    positions = query_idx - query_off
    rot_keys = rotate_flat(keys, positions, head_size).astype(jnp.bfloat16)
    width = queries.shape[1]
    chip_rows = lax.all_gather(
        jnp.concatenate([queries, keys, values], axis=1), "core", axis=0, tiled=True
    )
    chip_kv = chip_rows[:, width:]
    out_weight, chip_kv = lax.optimization_barrier((out_weight, chip_kv))
    if chips <= 8:
        reach = chips // 2
        mine = [list(range(1, reach + 1)), [chips - p for p in range(1, reach + 1)]]
        got = []
        for p in range(reach):
            pairs = []
            for i in range(chips):
                for k in range(cores):
                    pairs.append((i * cores + k, ((i + mine[k][p]) % chips) * cores + k))
            got.append(lax.ppermute(chip_kv, BLK, pairs))
        both = lax.all_gather(jnp.stack(got, 0), "core", axis=0, tiled=False)
        pieces = {0: chip_kv}
        for k in range(cores):
            for p in range(reach):
                pieces.setdefault(mine[k][p], both[k, p])
        kv_pair = jnp.concatenate([pieces[s] for s in range(chips)], axis=0)
        src_chip = (lax.axis_index("chip") - jnp.arange(chips)) % chips
    else:
        kv_pair = lax.all_gather(chip_kv, "chip", axis=0, tiled=True)
        src_chip = jnp.arange(chips)
    if chips <= 8:
        held = [out_weight] + [
            lax.ppermute(out_weight, "chip", [(i, (i + s) % chips) for i in range(chips)])
            for s in range(1, chips)
        ]
        back = jnp.stack(held[::-1] + held[::-1], axis=0)
        here = lax.axis_index("chip")
        w_share = lax.dynamic_slice_in_dim(back, chips - 1 - here, chips, 0).reshape(
            chips * out_weight.shape[0], out_weight.shape[1]
        )
    else:
        w_share = lax.all_gather(out_weight, "chip", axis=0, tiled=True)
    chip_q = chip_rows[:, :width]
    chip_tok = cores * tok_rows
    chip_idx = lax.axis_index("chip") * chip_tok + jnp.arange(chip_tok)
    chip_seg, chip_off = locate(chip_idx, starts)
    chip_q = rotate_flat(chip_q, chip_idx - chip_off, head_size).astype(jnp.bfloat16)
    query_rows = jnp.concatenate(
        [chip_q[:, h * head_size:(h + 1) * head_size] for h in range(groups)], axis=0
    )
    row_idx = jnp.tile(chip_idx, groups)
    row_seg = jnp.tile(chip_seg, groups)
    scale = 1.0 / head_size**0.5
    value_piece = kv_pair[:, head_size:]
    span = kv_pair.shape[0]
    chip_tok_kv = chip_kv.shape[0]
    key_idx = (src_chip[:, None] * chip_tok_kv + jnp.arange(chip_tok_kv)[None, :]).reshape(span)
    key_seg, key_off = locate(key_idx, starts)
    key_piece = rotate_flat(kv_pair[:, :head_size], key_idx - key_off, head_size).astype(
        jnp.bfloat16
    )
    key_piece, value_piece = lax.optimization_barrier((key_piece, value_piece))
    live = (key_seg[None, :] == row_seg[:, None]) & (key_idx[None, :] <= row_idx[:, None])
    scores = (
        jnp.einsum("rd,nd->rn", query_rows, key_piece, preferred_element_type=jnp.float32) * scale
    )
    scores = jnp.where(live, scores, -1e30)
    new_max = jnp.max(scores, axis=1)
    probs = jnp.where(live, jnp.exp(scores - new_max[:, None]), 0.0)
    new_sum = jnp.sum(probs, axis=1)
    new_weighted = jnp.dot(
        probs.astype(jnp.bfloat16), value_piece, preferred_element_type=jnp.float32
    )
    att_rows = (new_weighted / new_sum[:, None]).astype(jnp.bfloat16)
    chip_att = jnp.concatenate(
        [att_rows[h * chip_tok:(h + 1) * chip_tok] for h in range(groups)], axis=1
    )
    kvs = lax.axis_size("kv")
    per_c = w_share.shape[0] // kvs
    routed = jnp.stack(
        [
            jnp.dot(
                chip_att,
                w_share[c * per_c:(c + 1) * per_c].T,
                preferred_element_type=jnp.float32,
            ).astype(jnp.bfloat16)
            for c in range(kvs)
        ],
        axis=0,
    ).reshape(kvs * cores, tok_rows, per_c)
    got = lax.all_to_all(routed, ("kv", "core"), 0, 0, tiled=True)
    total = jnp.sum(got.reshape(kvs, cores, tok_rows, per_c).astype(jnp.float32), axis=0)
    rows = out_weight.shape[0]
    hidden = (
        total.reshape(cores, tok_rows, per_c // rows, rows)
        .transpose(1, 2, 0, 3)
        .reshape(tok_rows, cores * per_c)
        .astype(jnp.bfloat16)
    )
    return (hidden, rot_keys)


def solution(mesh):
    kv_size, blk_size = mesh.devices.shape
    sub = Mesh(mesh.devices.reshape(kv_size, blk_size // 2, 2), ("kv",) + BLK)
    return jax.shard_map(
        body,
        mesh=sub,
        in_specs=(P(BLK, "kv"), P(BLK, "kv"), P(BLK, "kv"), P(), P(BLK, "kv")),
        out_specs=(P(BLK, "kv"), P(BLK, "kv")),
        check_vma=False,
    )
```

```python
import jax
import jax.numpy as jnp
import numpy as np
from jax import lax
from jax.sharding import Mesh
from jax.sharding import PartitionSpec as P

rope_base = 500000.0
BLK = ("chip", "core")


def locate(index, starts):
    hit = starts[None, :] <= index[:, None]
    segment = jnp.sum(hit.astype(jnp.int32), axis=1) - 1
    offset = jnp.max(jnp.where(hit, starts[None, :], 0), axis=1)
    return (segment, offset)


def half_swap(width, head_size):
    half = head_size // 2
    col = np.arange(width)
    within = col % head_size
    src = np.where(within < half, col + half, col - half)
    sign = np.where(within < half, -1.0, 1.0)
    swap = np.zeros((width, width), np.float32)
    swap[src, col] = sign
    return jnp.asarray(swap, jnp.bfloat16)


def rotate_flat(field, positions, head_size):
    half = head_size // 2
    steps = jnp.arange(half).astype(jnp.float32) * (2.0 / head_size)
    inverse = jnp.power(jnp.float32(rope_base), -steps)
    angle = positions.astype(jnp.float32)[:, None] * inverse[None, :]
    reps = field.shape[1] // head_size
    cosine = jnp.tile(jnp.cos(angle), (1, 2 * reps))
    sine = jnp.tile(jnp.sin(angle), (1, 2 * reps))
    swapped = jnp.dot(
        field, half_swap(field.shape[1], head_size), preferred_element_type=jnp.float32
    )
    return field.astype(jnp.float32) * cosine + swapped * sine


def body(queries, keys, values, lengths, out_weight):
    tok_rows = queries.shape[0]
    head_size = keys.shape[1]
    groups = queries.shape[1] // head_size
    cores = lax.axis_size("core")
    chips = lax.axis_size("chip")
    total_len = tok_rows * chips * cores
    seg_id = jnp.arange(lengths.shape[0] + 1)[:, None]
    short_id = jnp.arange(lengths.shape[0])[None, :]
    tail = jnp.sum(jnp.where(short_id >= seg_id - 1, lengths[None, :], 0), axis=1)
    starts = jnp.where(seg_id[:, 0] == 0, 0, total_len - tail)
    blk_idx = lax.axis_index("chip") * cores + lax.axis_index("core")
    first_tok = blk_idx * tok_rows
    query_idx = first_tok + jnp.arange(tok_rows)
    query_seg, query_off = locate(query_idx, starts)
    positions = query_idx - query_off
    if chips <= 8:
        held = [out_weight] + [
            lax.ppermute(out_weight, "chip", [(i, (i + s) % chips) for i in range(chips)])
            for s in range(1, chips)
        ]
        back = jnp.stack(held[::-1] + held[::-1], axis=0)
        here = lax.axis_index("chip")
        w_share = lax.dynamic_slice_in_dim(back, chips - 1 - here, chips, 0).reshape(
            chips * out_weight.shape[0], out_weight.shape[1]
        )
    else:
        w_share = lax.all_gather(out_weight, "chip", axis=0, tiled=True)
    rot_keys = rotate_flat(keys, positions, head_size).astype(jnp.bfloat16)
    rot_queries = rotate_flat(queries, positions, head_size).astype(jnp.bfloat16)
    width = queries.shape[1]
    chip_rows = lax.all_gather(
        jnp.concatenate([rot_queries, rot_keys, values], axis=1), "core", axis=0, tiled=True
    )
    chip_kv = chip_rows[:, width:]
    if chips <= 8:
        kv_pair = jnp.concatenate(
            [chip_kv]
            + [
                lax.ppermute(chip_kv, "chip", [(i, (i + s) % chips) for i in range(chips)])
                for s in range(1, chips)
            ],
            axis=0,
        )
        src_chip = (lax.axis_index("chip") - jnp.arange(chips)) % chips
    else:
        kv_pair = lax.all_gather(chip_kv, "chip", axis=0, tiled=True)
        src_chip = jnp.arange(chips)
    chip_q = chip_rows[:, :width]
    chip_tok = cores * tok_rows
    chip_idx = lax.axis_index("chip") * chip_tok + jnp.arange(chip_tok)
    chip_seg, _ = locate(chip_idx, starts)
    query_rows = jnp.concatenate(
        [chip_q[:, h * head_size:(h + 1) * head_size] for h in range(groups)], axis=0
    )
    row_idx = jnp.tile(chip_idx, groups)
    row_seg = jnp.tile(chip_seg, groups)
    scale = 1.0 / head_size**0.5
    key_piece = kv_pair[:, :head_size]
    value_piece = kv_pair[:, head_size:]
    span = key_piece.shape[0]
    chip_tok_kv = chip_kv.shape[0]
    key_idx = (src_chip[:, None] * chip_tok_kv + jnp.arange(chip_tok_kv)[None, :]).reshape(span)
    key_seg, key_off = locate(key_idx, starts)
    live = (key_seg[None, :] == row_seg[:, None]) & (key_idx[None, :] <= row_idx[:, None])
    scores = (
        jnp.einsum("rd,nd->rn", query_rows, key_piece, preferred_element_type=jnp.float32) * scale
    )
    scores = jnp.where(live, scores, -1e30)
    new_max = jnp.max(scores, axis=1)
    probs = jnp.where(live, jnp.exp(scores - new_max[:, None]), 0.0)
    new_sum = jnp.sum(probs, axis=1)
    new_weighted = jnp.dot(
        probs.astype(jnp.bfloat16), value_piece, preferred_element_type=jnp.float32
    )
    att_rows = (new_weighted / new_sum[:, None]).astype(jnp.bfloat16)
    chip_att = jnp.concatenate(
        [att_rows[h * chip_tok:(h + 1) * chip_tok] for h in range(groups)], axis=1
    )
    kvs = lax.axis_size("kv")
    per_c = w_share.shape[0] // kvs
    routed = (
        jnp.einsum(
            "ctk,cnk->ctn",
            jnp.broadcast_to(chip_att, (kvs,) + chip_att.shape),
            w_share.reshape(kvs, per_c, w_share.shape[1]),
            preferred_element_type=jnp.float32,
        )
        .astype(jnp.bfloat16)
        .reshape(kvs * cores, tok_rows, per_c)
    )
    got = lax.all_to_all(routed, ("kv", "core"), 0, 0, tiled=True)
    total = jnp.sum(got.reshape(kvs, cores, tok_rows, per_c).astype(jnp.float32), axis=0)
    rows = out_weight.shape[0]
    if per_c == rows:
        hidden = jnp.concatenate([total[k] for k in range(cores)], axis=1).astype(jnp.bfloat16)
    else:
        hidden = (
            total.reshape(cores, tok_rows, per_c // rows, rows)
            .transpose(1, 2, 0, 3)
            .reshape(tok_rows, cores * per_c)
            .astype(jnp.bfloat16)
        )
    return (hidden, rot_keys)


def solution(mesh):
    kv_size, blk_size = mesh.devices.shape
    sub = Mesh(mesh.devices.reshape(kv_size, blk_size // 2, 2), ("kv",) + BLK)
    return jax.shard_map(
        body,
        mesh=sub,
        in_specs=(P(BLK, "kv"), P(BLK, "kv"), P(BLK, "kv"), P(), P(BLK, "kv")),
        out_specs=(P(BLK, "kv"), P(BLK, "kv")),
        check_vma=False,
    )
```

```python
import jax
import jax.numpy as jnp
import numpy as np
from jax import lax
from jax.sharding import Mesh
from jax.sharding import PartitionSpec as P

rope_base = 500000.0
BLK = ("chip", "core")


def locate(index, starts):
    hit = starts[None, :] <= index[:, None]
    segment = jnp.sum(hit.astype(jnp.int32), axis=1) - 1
    offset = jnp.max(jnp.where(hit, starts[None, :], 0), axis=1)
    return (segment, offset)


def half_swap(width, head_size):
    half = head_size // 2
    col = np.arange(width)
    within = col % head_size
    src = np.where(within < half, col + half, col - half)
    sign = np.where(within < half, -1.0, 1.0)
    swap = np.zeros((width, width), np.float32)
    swap[src, col] = sign
    return jnp.asarray(swap, jnp.bfloat16)


def rotate_flat(field, positions, head_size):
    half = head_size // 2
    steps = jnp.arange(half).astype(jnp.float32) * (2.0 / head_size)
    inverse = jnp.power(jnp.float32(rope_base), -steps)
    angle = positions.astype(jnp.float32)[:, None] * inverse[None, :]
    reps = field.shape[1] // head_size
    cosine = jnp.tile(jnp.cos(angle), (1, 2 * reps))
    sine = jnp.tile(jnp.sin(angle), (1, 2 * reps))
    swapped = jnp.dot(
        field, half_swap(field.shape[1], head_size), preferred_element_type=jnp.float32
    )
    return field.astype(jnp.float32) * cosine + swapped * sine


def body(queries, keys, values, lengths, out_weight):
    tok_rows = queries.shape[0]
    head_size = keys.shape[1]
    groups = queries.shape[1] // head_size
    cores = lax.axis_size("core")
    chips = lax.axis_size("chip")
    total_len = tok_rows * chips * cores
    seg_id = jnp.arange(lengths.shape[0] + 1)[:, None]
    short_id = jnp.arange(lengths.shape[0])[None, :]
    tail = jnp.sum(jnp.where(short_id >= seg_id - 1, lengths[None, :], 0), axis=1)
    starts = jnp.where(seg_id[:, 0] == 0, 0, total_len - tail)
    blk_idx = lax.axis_index("chip") * cores + lax.axis_index("core")
    first_tok = blk_idx * tok_rows
    query_idx = first_tok + jnp.arange(tok_rows)
    query_seg, query_off = locate(query_idx, starts)
    positions = query_idx - query_off
    if chips <= 8:
        held = [out_weight] + [
            lax.ppermute(out_weight, "chip", [(i, (i + s) % chips) for i in range(chips)])
            for s in range(1, chips)
        ]
        back = jnp.stack(held[::-1] + held[::-1], axis=0)
        here = lax.axis_index("chip")
        w_share = lax.dynamic_slice_in_dim(back, chips - 1 - here, chips, 0).reshape(
            chips * out_weight.shape[0], out_weight.shape[1]
        )
    else:
        w_share = lax.all_gather(out_weight, "chip", axis=0, tiled=True)
    rot_keys = rotate_flat(keys, positions, head_size).astype(jnp.bfloat16)
    rot_queries = rotate_flat(queries, positions, head_size).astype(jnp.bfloat16)
    width = queries.shape[1]
    chip_rows = lax.all_gather(
        jnp.concatenate([rot_queries, rot_keys, values], axis=1), "core", axis=0, tiled=True
    )
    chip_kv = chip_rows[:, width:]
    if chips <= 8:
        reach = chips // 2
        mine = [list(range(1, reach + 1)), [chips - p for p in range(1, reach + 1)]]
        fetched = []
        for p in range(reach):
            pairs = []
            for i in range(chips):
                for k in range(cores):
                    pairs.append((i * cores + k, ((i + mine[k][p]) % chips) * cores + k))
            fetched.append(lax.ppermute(chip_kv, BLK, pairs))
        both = lax.all_gather(jnp.stack(fetched, 0), "core", axis=0, tiled=False)
        pieces = {0: chip_kv}
        for k in range(cores):
            for p in range(reach):
                pieces.setdefault(mine[k][p], both[k, p])
        kv_pair = jnp.concatenate([pieces[s] for s in range(chips)], axis=0)
        src_chip = (lax.axis_index("chip") - jnp.arange(chips)) % chips
    else:
        kv_pair = lax.all_gather(chip_kv, "chip", axis=0, tiled=True)
        src_chip = jnp.arange(chips)
    chip_q = chip_rows[:, :width]
    chip_tok = cores * tok_rows
    chip_idx = lax.axis_index("chip") * chip_tok + jnp.arange(chip_tok)
    chip_seg, _ = locate(chip_idx, starts)
    query_rows = jnp.concatenate(
        [chip_q[:, h * head_size:(h + 1) * head_size] for h in range(groups)], axis=0
    )
    row_idx = jnp.tile(chip_idx, groups)
    row_seg = jnp.tile(chip_seg, groups)
    scale = 1.0 / head_size**0.5
    key_piece = kv_pair[:, :head_size]
    value_piece = kv_pair[:, head_size:]
    span = key_piece.shape[0]
    chip_tok_kv = chip_kv.shape[0]
    key_idx = (src_chip[:, None] * chip_tok_kv + jnp.arange(chip_tok_kv)[None, :]).reshape(span)
    key_seg, key_off = locate(key_idx, starts)
    live = (key_seg[None, :] == row_seg[:, None]) & (key_idx[None, :] <= row_idx[:, None])
    scores = (
        jnp.einsum("rd,nd->rn", query_rows, key_piece, preferred_element_type=jnp.float32) * scale
    )
    scores = jnp.where(live, scores, -1e30)
    new_max = jnp.max(scores, axis=1)
    probs = jnp.where(live, jnp.exp(scores - new_max[:, None]), 0.0)
    new_sum = jnp.sum(probs, axis=1)
    new_weighted = jnp.dot(
        probs.astype(jnp.bfloat16), value_piece, preferred_element_type=jnp.float32
    )
    att_rows = (new_weighted / new_sum[:, None]).astype(jnp.bfloat16)
    chip_att = jnp.concatenate(
        [att_rows[h * chip_tok:(h + 1) * chip_tok] for h in range(groups)], axis=1
    )
    kvs = lax.axis_size("kv")
    per_c = w_share.shape[0] // kvs
    routed = (
        jnp.einsum(
            "ctk,cnk->ctn",
            jnp.broadcast_to(chip_att, (kvs,) + chip_att.shape),
            w_share.reshape(kvs, per_c, w_share.shape[1]),
            preferred_element_type=jnp.float32,
        )
        .astype(jnp.bfloat16)
        .reshape(kvs * cores, tok_rows, per_c)
    )
    got = lax.all_to_all(routed, ("kv", "core"), 0, 0, tiled=True)
    total = jnp.sum(got.reshape(kvs, cores, tok_rows, per_c).astype(jnp.float32), axis=0)
    rows = out_weight.shape[0]
    if per_c == rows:
        hidden = jnp.concatenate([total[k] for k in range(cores)], axis=1).astype(jnp.bfloat16)
    else:
        hidden = (
            total.reshape(cores, tok_rows, per_c // rows, rows)
            .transpose(1, 2, 0, 3)
            .reshape(tok_rows, cores * per_c)
            .astype(jnp.bfloat16)
        )
    return (hidden, rot_keys)


def solution(mesh):
    kv_size, blk_size = mesh.devices.shape
    sub = Mesh(mesh.devices.reshape(kv_size, blk_size // 2, 2), ("kv",) + BLK)
    return jax.shard_map(
        body,
        mesh=sub,
        in_specs=(P(BLK, "kv"), P(BLK, "kv"), P(BLK, "kv"), P(), P(BLK, "kv")),
        out_specs=(P(BLK, "kv"), P(BLK, "kv")),
        check_vma=False,
    )
```

```python
import jax
import jax.numpy as jnp
import numpy as np
from jax import lax
from jax.sharding import Mesh
from jax.sharding import PartitionSpec as P

rope_base = 500000.0
BLK = ("chip", "core")


def locate(index, starts):
    hit = starts[None, :] <= index[:, None]
    segment = jnp.sum(hit.astype(jnp.int32), axis=1) - 1
    offset = jnp.max(jnp.where(hit, starts[None, :], 0), axis=1)
    return (segment, offset)


def half_swap(width, head_size):
    half = head_size // 2
    col = np.arange(width)
    within = col % head_size
    src = np.where(within < half, col + half, col - half)
    sign = np.where(within < half, -1.0, 1.0)
    swap = np.zeros((width, width), np.float32)
    swap[src, col] = sign
    return jnp.asarray(swap, jnp.bfloat16)


def rotate_flat(field, positions, head_size):
    half = head_size // 2
    steps = jnp.arange(half).astype(jnp.float32) * (2.0 / head_size)
    inverse = jnp.power(jnp.float32(rope_base), -steps)
    angle = positions.astype(jnp.float32)[:, None] * inverse[None, :]
    reps = field.shape[1] // head_size
    cosine = jnp.tile(jnp.cos(angle), (1, 2 * reps))
    sine = jnp.tile(jnp.sin(angle), (1, 2 * reps))
    swapped = jnp.dot(
        field, half_swap(field.shape[1], head_size), preferred_element_type=jnp.float32
    )
    return field.astype(jnp.float32) * cosine + swapped * sine


def body(queries, keys, values, lengths, out_weight):
    tok_rows = queries.shape[0]
    head_size = keys.shape[1]
    groups = queries.shape[1] // head_size
    cores = lax.axis_size("core")
    chips = lax.axis_size("chip")
    total_len = tok_rows * chips * cores
    seg_id = jnp.arange(lengths.shape[0] + 1)[:, None]
    short_id = jnp.arange(lengths.shape[0])[None, :]
    tail = jnp.sum(jnp.where(short_id >= seg_id - 1, lengths[None, :], 0), axis=1)
    starts = jnp.where(seg_id[:, 0] == 0, 0, total_len - tail)
    blk_idx = lax.axis_index("chip") * cores + lax.axis_index("core")
    first_tok = blk_idx * tok_rows
    query_idx = first_tok + jnp.arange(tok_rows)
    query_seg, query_off = locate(query_idx, starts)
    positions = query_idx - query_off
    kvs = lax.axis_size("kv")
    xor_plan = chips == 4 and kvs == chips
    if xor_plan:
        w_x = lax.ppermute(out_weight, "chip", [(i, i ^ 1) for i in range(chips)])
        w_y = lax.ppermute(out_weight, "chip", [(i, i ^ 2) for i in range(chips)])
    elif chips <= 8:
        held = [out_weight] + [
            lax.ppermute(out_weight, "chip", [(i, (i + s) % chips) for i in range(chips)])
            for s in range(1, chips)
        ]
        back = jnp.stack(held[::-1] + held[::-1], axis=0)
        here = lax.axis_index("chip")
        w_share = lax.dynamic_slice_in_dim(back, chips - 1 - here, chips, 0).reshape(
            chips * out_weight.shape[0], out_weight.shape[1]
        )
    else:
        w_share = lax.all_gather(out_weight, "chip", axis=0, tiled=True)
    rot_keys = rotate_flat(keys, positions, head_size).astype(jnp.bfloat16)
    rot_queries = rotate_flat(queries, positions, head_size).astype(jnp.bfloat16)
    width = queries.shape[1]
    chip_rows = lax.all_gather(
        jnp.concatenate([rot_queries, rot_keys, values], axis=1), "core", axis=0, tiled=True
    )
    chip_kv = chip_rows[:, width:]
    if chips <= 8:
        reach = chips // 2
        mine = [list(range(1, reach + 1)), [chips - p for p in range(1, reach + 1)]]
        fetched = []
        for p in range(reach):
            pairs = []
            for i in range(chips):
                for k in range(cores):
                    pairs.append((i * cores + k, ((i + mine[k][p]) % chips) * cores + k))
            fetched.append(lax.ppermute(chip_kv, BLK, pairs))
        both = lax.all_gather(jnp.stack(fetched, 0), "core", axis=0, tiled=False)
        pieces = {0: chip_kv}
        for k in range(cores):
            for p in range(reach):
                pieces.setdefault(mine[k][p], both[k, p])
        kv_pair = jnp.concatenate([pieces[s] for s in range(chips)], axis=0)
        src_chip = (lax.axis_index("chip") - jnp.arange(chips)) % chips
    else:
        kv_pair = lax.all_gather(chip_kv, "chip", axis=0, tiled=True)
        src_chip = jnp.arange(chips)
    chip_q = chip_rows[:, :width]
    chip_tok = cores * tok_rows
    chip_idx = lax.axis_index("chip") * chip_tok + jnp.arange(chip_tok)
    chip_seg, _ = locate(chip_idx, starts)
    query_rows = jnp.concatenate(
        [chip_q[:, h * head_size:(h + 1) * head_size] for h in range(groups)], axis=0
    )
    row_idx = jnp.tile(chip_idx, groups)
    row_seg = jnp.tile(chip_seg, groups)
    scale = 1.0 / head_size**0.5
    key_piece = kv_pair[:, :head_size]
    value_piece = kv_pair[:, head_size:]
    span = key_piece.shape[0]
    chip_tok_kv = chip_kv.shape[0]
    key_idx = (src_chip[:, None] * chip_tok_kv + jnp.arange(chip_tok_kv)[None, :]).reshape(span)
    key_seg, key_off = locate(key_idx, starts)
    live = (key_seg[None, :] == row_seg[:, None]) & (key_idx[None, :] <= row_idx[:, None])
    scores = (
        jnp.einsum("rd,nd->rn", query_rows, key_piece, preferred_element_type=jnp.float32) * scale
    )
    scores = jnp.where(live, scores, -1e30)
    new_max = jnp.max(scores, axis=1)
    probs = jnp.where(live, jnp.exp(scores - new_max[:, None]), 0.0)
    new_sum = jnp.sum(probs, axis=1)
    new_weighted = jnp.dot(
        probs.astype(jnp.bfloat16), value_piece, preferred_element_type=jnp.float32
    )
    att_rows = (new_weighted / new_sum[:, None]).astype(jnp.bfloat16)
    chip_att = jnp.concatenate(
        [att_rows[h * chip_tok:(h + 1) * chip_tok] for h in range(groups)], axis=1
    )
    if xor_plan:
        per_c = out_weight.shape[0]

        def part(att, w):
            return jnp.dot(att, w.T, preferred_element_type=jnp.float32).astype(jnp.bfloat16)

        att_x = lax.ppermute(chip_att, "chip", [(i, i ^ 1) for i in range(chips)])
        diag = lax.ppermute(part(att_x, w_y), "chip", [(i, i ^ 1) for i in range(chips)])
        by_dist = jnp.stack([part(chip_att, out_weight), part(chip_att, w_x), part(chip_att, w_y), diag])
        here = lax.axis_index("chip")
        routed = jnp.stack(
            [lax.dynamic_index_in_dim(by_dist, here ^ c, 0, keepdims=False) for c in range(kvs)]
        ).reshape(kvs * cores, tok_rows, per_c)
    else:
        per_c = w_share.shape[0] // kvs
        routed = (
            jnp.einsum(
                "ctk,cnk->ctn",
                jnp.broadcast_to(chip_att, (kvs,) + chip_att.shape),
                w_share.reshape(kvs, per_c, w_share.shape[1]),
                preferred_element_type=jnp.float32,
            )
            .astype(jnp.bfloat16)
            .reshape(kvs * cores, tok_rows, per_c)
        )
    got = lax.all_to_all(routed, ("kv", "core"), 0, 0, tiled=True)
    total = jnp.sum(got.reshape(kvs, cores, tok_rows, per_c).astype(jnp.float32), axis=0)
    rows = out_weight.shape[0]
    if per_c == rows:
        hidden = jnp.concatenate([total[k] for k in range(cores)], axis=1).astype(jnp.bfloat16)
    else:
        hidden = (
            total.reshape(cores, tok_rows, per_c // rows, rows)
            .transpose(1, 2, 0, 3)
            .reshape(tok_rows, cores * per_c)
            .astype(jnp.bfloat16)
        )
    return (hidden, rot_keys)


def solution(mesh):
    kv_size, blk_size = mesh.devices.shape
    sub = Mesh(mesh.devices.reshape(kv_size, blk_size // 2, 2), ("kv",) + BLK)
    return jax.shard_map(
        body,
        mesh=sub,
        in_specs=(P(BLK, "kv"), P(BLK, "kv"), P(BLK, "kv"), P(), P(BLK, "kv")),
        out_specs=(P(BLK, "kv"), P(BLK, "kv")),
        check_vma=False,
    )
```

```python
import jax
import jax.numpy as jnp
import numpy as np
from jax import lax
from jax.sharding import Mesh
from jax.sharding import PartitionSpec as P

rope_base = 500000.0
BLK = ("chip", "core")


def locate(index, starts):
    hit = starts[None, :] <= index[:, None]
    segment = jnp.sum(hit.astype(jnp.int32), axis=1) - 1
    offset = jnp.max(jnp.where(hit, starts[None, :], 0), axis=1)
    return (segment, offset)


def half_swap(width, head_size):
    half = head_size // 2
    col = np.arange(width)
    within = col % head_size
    src = np.where(within < half, col + half, col - half)
    sign = np.where(within < half, -1.0, 1.0)
    swap = np.zeros((width, width), np.float32)
    swap[src, col] = sign
    return jnp.asarray(swap, jnp.bfloat16)


def rotate_flat(field, positions, head_size):
    half = head_size // 2
    steps = jnp.arange(half).astype(jnp.float32) * (2.0 / head_size)
    inverse = jnp.power(jnp.float32(rope_base), -steps)
    angle = positions.astype(jnp.float32)[:, None] * inverse[None, :]
    reps = field.shape[1] // head_size
    cosine = jnp.tile(jnp.cos(angle), (1, 2 * reps))
    sine = jnp.tile(jnp.sin(angle), (1, 2 * reps))
    swapped = jnp.dot(
        field, half_swap(field.shape[1], head_size), preferred_element_type=jnp.float32
    )
    return field.astype(jnp.float32) * cosine + swapped * sine


def body(queries, keys, values, lengths, out_weight):
    tok_rows = queries.shape[0]
    head_size = keys.shape[1]
    groups = queries.shape[1] // head_size
    cores = lax.axis_size("core")
    chips = lax.axis_size("chip")
    total_len = tok_rows * chips * cores
    seg_id = jnp.arange(lengths.shape[0] + 1)[:, None]
    short_id = jnp.arange(lengths.shape[0])[None, :]
    tail = jnp.sum(jnp.where(short_id >= seg_id - 1, lengths[None, :], 0), axis=1)
    starts = jnp.where(seg_id[:, 0] == 0, 0, total_len - tail)
    blk_idx = lax.axis_index("chip") * cores + lax.axis_index("core")
    first_tok = blk_idx * tok_rows
    query_idx = first_tok + jnp.arange(tok_rows)
    query_seg, query_off = locate(query_idx, starts)
    positions = query_idx - query_off
    kvs = lax.axis_size("kv")
    xor_plan = chips == 4 and kvs == chips
    if xor_plan:
        w_x = lax.ppermute(out_weight, "chip", [(i, i ^ 1) for i in range(chips)])
        w_y = lax.ppermute(out_weight, "chip", [(i, i ^ 2) for i in range(chips)])
    elif chips <= 8:
        held = [out_weight] + [
            lax.ppermute(out_weight, "chip", [(i, (i + s) % chips) for i in range(chips)])
            for s in range(1, chips)
        ]
        back = jnp.stack(held[::-1] + held[::-1], axis=0)
        here = lax.axis_index("chip")
        w_share = lax.dynamic_slice_in_dim(back, chips - 1 - here, chips, 0).reshape(
            chips * out_weight.shape[0], out_weight.shape[1]
        )
    else:
        w_share = lax.all_gather(out_weight, "chip", axis=0, tiled=True)
    rot_keys = rotate_flat(keys, positions, head_size).astype(jnp.bfloat16)
    rot_queries = rotate_flat(queries, positions, head_size).astype(jnp.bfloat16)
    width = queries.shape[1]
    chip_rows = lax.all_gather(
        jnp.concatenate([rot_queries, rot_keys, values], axis=1), "core", axis=0, tiled=True
    )
    chip_kv = chip_rows[:, width:]
    if chips <= 8:
        reach = chips // 2
        mine = [list(range(1, reach + 1)), [chips - p for p in range(1, reach + 1)]]
        fetched = []
        for p in range(reach):
            pairs = []
            for i in range(chips):
                for k in range(cores):
                    pairs.append((i * cores + k, ((i + mine[k][p]) % chips) * cores + k))
            fetched.append(lax.ppermute(chip_kv, BLK, pairs))
        both = lax.all_gather(jnp.stack(fetched, 0), "core", axis=0, tiled=False)
        pieces = {0: chip_kv}
        for k in range(cores):
            for p in range(reach):
                pieces.setdefault(mine[k][p], both[k, p])
        kv_pair = jnp.concatenate([pieces[s] for s in range(chips)], axis=0)
        src_chip = (lax.axis_index("chip") - jnp.arange(chips)) % chips
    else:
        kv_pair = lax.all_gather(chip_kv, "chip", axis=0, tiled=True)
        src_chip = jnp.arange(chips)
    chip_q = chip_rows[:, :width]
    chip_tok = cores * tok_rows
    chip_idx = lax.axis_index("chip") * chip_tok + jnp.arange(chip_tok)
    chip_seg, _ = locate(chip_idx, starts)
    query_rows = jnp.concatenate(
        [chip_q[:, h * head_size:(h + 1) * head_size] for h in range(groups)], axis=0
    )
    row_idx = jnp.tile(chip_idx, groups)
    row_seg = jnp.tile(chip_seg, groups)
    scale = 1.0 / head_size**0.5
    key_piece = kv_pair[:, :head_size]
    value_piece = kv_pair[:, head_size:]
    span = key_piece.shape[0]
    chip_tok_kv = chip_kv.shape[0]
    key_idx = (src_chip[:, None] * chip_tok_kv + jnp.arange(chip_tok_kv)[None, :]).reshape(span)
    key_seg, key_off = locate(key_idx, starts)
    live = (key_seg[None, :] == row_seg[:, None]) & (key_idx[None, :] <= row_idx[:, None])
    scores = (
        jnp.einsum("rd,nd->rn", query_rows, key_piece, preferred_element_type=jnp.float32) * scale
    )
    scores = jnp.where(live, scores, -1e30)
    new_max = jnp.max(scores, axis=1)
    probs = jnp.where(live, jnp.exp(scores - new_max[:, None]), 0.0)
    new_sum = jnp.sum(probs, axis=1)
    new_weighted = jnp.dot(
        probs.astype(jnp.bfloat16), value_piece, preferred_element_type=jnp.float32
    )
    att_rows = (new_weighted / new_sum[:, None]).astype(jnp.bfloat16)
    chip_att = jnp.concatenate(
        [att_rows[h * chip_tok:(h + 1) * chip_tok] for h in range(groups)], axis=1
    )
    if xor_plan:
        per_c = out_weight.shape[0]

        def part(att, w):
            return jnp.dot(att, w.T, preferred_element_type=jnp.float32).astype(jnp.bfloat16)

        w_x, w_y, chip_att = lax.optimization_barrier((w_x, w_y, chip_att))
        att_x = lax.ppermute(chip_att, "chip", [(i, i ^ 1) for i in range(chips)])
        diag = lax.ppermute(part(att_x, w_y), "chip", [(i, i ^ 1) for i in range(chips)])
        by_dist = jnp.stack([part(chip_att, out_weight), part(chip_att, w_x), part(chip_att, w_y), diag])
        here = lax.axis_index("chip")
        routed = jnp.stack(
            [lax.dynamic_index_in_dim(by_dist, here ^ c, 0, keepdims=False) for c in range(kvs)]
        ).reshape(kvs * cores, tok_rows, per_c)
    else:
        per_c = w_share.shape[0] // kvs
        routed = (
            jnp.einsum(
                "ctk,cnk->ctn",
                jnp.broadcast_to(chip_att, (kvs,) + chip_att.shape),
                w_share.reshape(kvs, per_c, w_share.shape[1]),
                preferred_element_type=jnp.float32,
            )
            .astype(jnp.bfloat16)
            .reshape(kvs * cores, tok_rows, per_c)
        )
    got = lax.all_to_all(routed, ("kv", "core"), 0, 0, tiled=True)
    total = jnp.sum(got.reshape(kvs, cores, tok_rows, per_c).astype(jnp.float32), axis=0)
    rows = out_weight.shape[0]
    if per_c == rows:
        hidden = jnp.concatenate([total[k] for k in range(cores)], axis=1).astype(jnp.bfloat16)
    else:
        hidden = (
            total.reshape(cores, tok_rows, per_c // rows, rows)
            .transpose(1, 2, 0, 3)
            .reshape(tok_rows, cores * per_c)
            .astype(jnp.bfloat16)
        )
    return (hidden, rot_keys)


def solution(mesh):
    kv_size, blk_size = mesh.devices.shape
    sub = Mesh(mesh.devices.reshape(kv_size, blk_size // 2, 2), ("kv",) + BLK)
    return jax.shard_map(
        body,
        mesh=sub,
        in_specs=(P(BLK, "kv"), P(BLK, "kv"), P(BLK, "kv"), P(), P(BLK, "kv")),
        out_specs=(P(BLK, "kv"), P(BLK, "kv")),
        check_vma=False,
    )
```

```python
import jax
import jax.numpy as jnp
import numpy as np
from jax import lax
from jax.sharding import Mesh
from jax.sharding import PartitionSpec as P

rope_base = 500000.0
BLK = ("chip", "core")


def locate(index, starts):
    hit = starts[None, :] <= index[:, None]
    segment = jnp.sum(hit.astype(jnp.int32), axis=1) - 1
    offset = jnp.max(jnp.where(hit, starts[None, :], 0), axis=1)
    return (segment, offset)


def half_swap(width, head_size):
    half = head_size // 2
    col = np.arange(width)
    within = col % head_size
    src = np.where(within < half, col + half, col - half)
    sign = np.where(within < half, -1.0, 1.0)
    swap = np.zeros((width, width), np.float32)
    swap[src, col] = sign
    return jnp.asarray(swap, jnp.bfloat16)


def rotate_flat(field, positions, head_size):
    half = head_size // 2
    steps = jnp.arange(half).astype(jnp.float32) * (2.0 / head_size)
    inverse = jnp.power(jnp.float32(rope_base), -steps)
    angle = positions.astype(jnp.float32)[:, None] * inverse[None, :]
    reps = field.shape[1] // head_size
    cosine = jnp.tile(jnp.cos(angle), (1, 2 * reps))
    sine = jnp.tile(jnp.sin(angle), (1, 2 * reps))
    swapped = jnp.dot(
        field, half_swap(field.shape[1], head_size), preferred_element_type=jnp.float32
    )
    return field.astype(jnp.float32) * cosine + swapped * sine


def body(queries, keys, values, lengths, out_weight):
    tok_rows = queries.shape[0]
    head_size = keys.shape[1]
    groups = queries.shape[1] // head_size
    cores = lax.axis_size("core")
    chips = lax.axis_size("chip")
    total_len = tok_rows * chips * cores
    seg_id = jnp.arange(lengths.shape[0] + 1)[:, None]
    short_id = jnp.arange(lengths.shape[0])[None, :]
    tail = jnp.sum(jnp.where(short_id >= seg_id - 1, lengths[None, :], 0), axis=1)
    starts = jnp.where(seg_id[:, 0] == 0, 0, total_len - tail)
    blk_idx = lax.axis_index("chip") * cores + lax.axis_index("core")
    first_tok = blk_idx * tok_rows
    query_idx = first_tok + jnp.arange(tok_rows)
    query_seg, query_off = locate(query_idx, starts)
    positions = query_idx - query_off
    kvs = lax.axis_size("kv")
    xor_plan = chips == 4 and kvs == chips
    if xor_plan:
        w_x = lax.ppermute(out_weight, "chip", [(i, i ^ 1) for i in range(chips)])
        w_y = lax.ppermute(out_weight, "chip", [(i, i ^ 2) for i in range(chips)])
    elif chips <= 8:
        held = [out_weight] + [
            lax.ppermute(out_weight, "chip", [(i, (i + s) % chips) for i in range(chips)])
            for s in range(1, chips)
        ]
        back = jnp.stack(held[::-1] + held[::-1], axis=0)
        here = lax.axis_index("chip")
        w_share = lax.dynamic_slice_in_dim(back, chips - 1 - here, chips, 0).reshape(
            chips * out_weight.shape[0], out_weight.shape[1]
        )
    else:
        w_share = lax.all_gather(out_weight, "chip", axis=0, tiled=True)
    rot_keys = rotate_flat(keys, positions, head_size).astype(jnp.bfloat16)
    rot_queries = rotate_flat(queries, positions, head_size).astype(jnp.bfloat16)
    width = queries.shape[1]
    chip_rows = lax.all_gather(
        jnp.concatenate([rot_queries, rot_keys, values], axis=1), "core", axis=0, tiled=True
    )
    chip_kv = chip_rows[:, width:]
    if chips <= 8:
        reach = chips // 2
        mine = [list(range(1, reach + 1)), [chips - p for p in range(1, reach + 1)]]
        fetched = []
        for p in range(reach):
            pairs = []
            for i in range(chips):
                for k in range(cores):
                    pairs.append((i * cores + k, ((i + mine[k][p]) % chips) * cores + k))
            fetched.append(lax.ppermute(chip_kv, BLK, pairs))
        both = lax.all_gather(jnp.stack(fetched, 0), "core", axis=0, tiled=False)
        pieces = {0: chip_kv}
        for k in range(cores):
            for p in range(reach):
                pieces.setdefault(mine[k][p], both[k, p])
        kv_pair = jnp.concatenate([pieces[s] for s in range(chips)], axis=0)
        src_chip = (lax.axis_index("chip") - jnp.arange(chips)) % chips
    else:
        kv_pair = lax.all_gather(chip_kv, "chip", axis=0, tiled=True)
        src_chip = jnp.arange(chips)
    chip_q = chip_rows[:, :width]
    chip_tok = cores * tok_rows
    chip_idx = lax.axis_index("chip") * chip_tok + jnp.arange(chip_tok)
    chip_seg, _ = locate(chip_idx, starts)
    query_rows = jnp.concatenate(
        [chip_q[:, h * head_size:(h + 1) * head_size] for h in range(groups)], axis=0
    )
    row_idx = jnp.tile(chip_idx, groups)
    row_seg = jnp.tile(chip_seg, groups)
    scale = 1.0 / head_size**0.5
    key_piece = kv_pair[:, :head_size]
    value_piece = kv_pair[:, head_size:]
    span = key_piece.shape[0]
    chip_tok_kv = chip_kv.shape[0]
    key_idx = (src_chip[:, None] * chip_tok_kv + jnp.arange(chip_tok_kv)[None, :]).reshape(span)
    key_seg, key_off = locate(key_idx, starts)
    live = (key_seg[None, :] == row_seg[:, None]) & (key_idx[None, :] <= row_idx[:, None])
    scores = (
        jnp.einsum("rd,nd->rn", query_rows, key_piece, preferred_element_type=jnp.float32) * scale
    )
    scores = jnp.where(live, scores, -1e30)
    new_max = jnp.max(scores, axis=1)
    probs = jnp.where(live, jnp.exp(scores - new_max[:, None]), 0.0)
    new_sum = jnp.sum(probs, axis=1)
    new_weighted = jnp.dot(
        probs.astype(jnp.bfloat16), value_piece, preferred_element_type=jnp.float32
    )
    att_rows = (new_weighted / new_sum[:, None]).astype(jnp.bfloat16)
    chip_att = jnp.concatenate(
        [att_rows[h * chip_tok:(h + 1) * chip_tok] for h in range(groups)], axis=1
    )
    if xor_plan:
        per_c = out_weight.shape[0]

        def part(att, w):
            return jnp.dot(att, w.T, preferred_element_type=jnp.float32).astype(jnp.bfloat16)

        att_x = lax.ppermute(chip_att, "chip", [(i, i ^ 1) for i in range(chips)])
        w_x, w_y, att_x = lax.optimization_barrier((w_x, w_y, att_x))
        diag = lax.ppermute(part(att_x, w_y), "chip", [(i, i ^ 1) for i in range(chips)])
        by_dist = jnp.stack([part(chip_att, out_weight), part(chip_att, w_x), part(chip_att, w_y), diag])
        here = lax.axis_index("chip")
        routed = jnp.stack(
            [lax.dynamic_index_in_dim(by_dist, here ^ c, 0, keepdims=False) for c in range(kvs)]
        ).reshape(kvs * cores, tok_rows, per_c)
    else:
        per_c = w_share.shape[0] // kvs
        routed = (
            jnp.einsum(
                "ctk,cnk->ctn",
                jnp.broadcast_to(chip_att, (kvs,) + chip_att.shape),
                w_share.reshape(kvs, per_c, w_share.shape[1]),
                preferred_element_type=jnp.float32,
            )
            .astype(jnp.bfloat16)
            .reshape(kvs * cores, tok_rows, per_c)
        )
    got = lax.all_to_all(routed, ("kv", "core"), 0, 0, tiled=True)
    total = jnp.sum(got.reshape(kvs, cores, tok_rows, per_c).astype(jnp.float32), axis=0)
    rows = out_weight.shape[0]
    if per_c == rows:
        hidden = jnp.concatenate([total[k] for k in range(cores)], axis=1).astype(jnp.bfloat16)
    else:
        hidden = (
            total.reshape(cores, tok_rows, per_c // rows, rows)
            .transpose(1, 2, 0, 3)
            .reshape(tok_rows, cores * per_c)
            .astype(jnp.bfloat16)
        )
    return (hidden, rot_keys)


def solution(mesh):
    kv_size, blk_size = mesh.devices.shape
    sub = Mesh(mesh.devices.reshape(kv_size, blk_size // 2, 2), ("kv",) + BLK)
    return jax.shard_map(
        body,
        mesh=sub,
        in_specs=(P(BLK, "kv"), P(BLK, "kv"), P(BLK, "kv"), P(), P(BLK, "kv")),
        out_specs=(P(BLK, "kv"), P(BLK, "kv")),
        check_vma=False,
    )
```

```python
import jax
import jax.numpy as jnp
import numpy as np
from jax import lax
from jax.sharding import Mesh
from jax.sharding import PartitionSpec as P

rope_base = 500000.0
BLK = ("chip", "core")


def locate(index, starts):
    hit = starts[None, :] <= index[:, None]
    segment = jnp.sum(hit.astype(jnp.int32), axis=1) - 1
    offset = jnp.max(jnp.where(hit, starts[None, :], 0), axis=1)
    return (segment, offset)


def half_swap(width, head_size):
    half = head_size // 2
    col = np.arange(width)
    within = col % head_size
    src = np.where(within < half, col + half, col - half)
    sign = np.where(within < half, -1.0, 1.0)
    swap = np.zeros((width, width), np.float32)
    swap[src, col] = sign
    return jnp.asarray(swap, jnp.bfloat16)


def rotate_flat(field, positions, head_size):
    half = head_size // 2
    steps = jnp.arange(half).astype(jnp.float32) * (2.0 / head_size)
    inverse = jnp.power(jnp.float32(rope_base), -steps)
    angle = positions.astype(jnp.float32)[:, None] * inverse[None, :]
    reps = field.shape[1] // head_size
    cosine = jnp.tile(jnp.cos(angle), (1, 2 * reps))
    sine = jnp.tile(jnp.sin(angle), (1, 2 * reps))
    swapped = jnp.dot(
        field, half_swap(field.shape[1], head_size), preferred_element_type=jnp.float32
    )
    return field.astype(jnp.float32) * cosine + swapped * sine


def body(queries, keys, values, lengths, out_weight):
    tok_rows = queries.shape[0]
    head_size = keys.shape[1]
    groups = queries.shape[1] // head_size
    cores = lax.axis_size("core")
    chips = lax.axis_size("chip")
    total_len = tok_rows * chips * cores
    seg_id = jnp.arange(lengths.shape[0] + 1)[:, None]
    short_id = jnp.arange(lengths.shape[0])[None, :]
    tail = jnp.sum(jnp.where(short_id >= seg_id - 1, lengths[None, :], 0), axis=1)
    starts = jnp.where(seg_id[:, 0] == 0, 0, total_len - tail)
    blk_idx = lax.axis_index("chip") * cores + lax.axis_index("core")
    first_tok = blk_idx * tok_rows
    query_idx = first_tok + jnp.arange(tok_rows)
    query_seg, query_off = locate(query_idx, starts)
    positions = query_idx - query_off
    kvs = lax.axis_size("kv")
    xor_plan = chips == 4 and kvs == chips
    if xor_plan:
        w_x = lax.ppermute(out_weight, "chip", [(i, i ^ 1) for i in range(chips)])
        w_y = lax.ppermute(out_weight, "chip", [(i, i ^ 2) for i in range(chips)])
    elif chips <= 8:
        held = [out_weight] + [
            lax.ppermute(out_weight, "chip", [(i, (i + s) % chips) for i in range(chips)])
            for s in range(1, chips)
        ]
        back = jnp.stack(held[::-1] + held[::-1], axis=0)
        here = lax.axis_index("chip")
        w_share = lax.dynamic_slice_in_dim(back, chips - 1 - here, chips, 0).reshape(
            chips * out_weight.shape[0], out_weight.shape[1]
        )
    else:
        w_share = lax.all_gather(out_weight, "chip", axis=0, tiled=True)
    rot_keys = rotate_flat(keys, positions, head_size).astype(jnp.bfloat16)
    rot_queries = rotate_flat(queries, positions, head_size).astype(jnp.bfloat16)
    width = queries.shape[1]
    chip_rows = lax.all_gather(
        jnp.concatenate([rot_queries, rot_keys, values], axis=1), "core", axis=0, tiled=True
    )
    chip_kv = chip_rows[:, width:]
    if chips <= 8:
        reach = chips // 2
        mine = [list(range(1, reach + 1)), [chips - p for p in range(1, reach + 1)]]
        fetched = []
        for p in range(reach):
            pairs = []
            for i in range(chips):
                for k in range(cores):
                    pairs.append((i * cores + k, ((i + mine[k][p]) % chips) * cores + k))
            fetched.append(lax.ppermute(chip_kv, BLK, pairs))
        both = lax.all_gather(jnp.stack(fetched, 0), "core", axis=0, tiled=False)
        pieces = {0: chip_kv}
        for k in range(cores):
            for p in range(reach):
                pieces.setdefault(mine[k][p], both[k, p])
        kv_pair = jnp.concatenate([pieces[s] for s in range(chips)], axis=0)
        src_chip = (lax.axis_index("chip") - jnp.arange(chips)) % chips
    else:
        kv_pair = lax.all_gather(chip_kv, "chip", axis=0, tiled=True)
        src_chip = jnp.arange(chips)
    chip_q = chip_rows[:, :width]
    chip_tok = cores * tok_rows
    chip_idx = lax.axis_index("chip") * chip_tok + jnp.arange(chip_tok)
    chip_seg, _ = locate(chip_idx, starts)
    query_rows = jnp.concatenate(
        [chip_q[:, h * head_size:(h + 1) * head_size] for h in range(groups)], axis=0
    )
    row_idx = jnp.tile(chip_idx, groups)
    row_seg = jnp.tile(chip_seg, groups)
    scale = 1.0 / head_size**0.5
    key_piece = kv_pair[:, :head_size]
    value_piece = kv_pair[:, head_size:]
    span = key_piece.shape[0]
    chip_tok_kv = chip_kv.shape[0]
    key_idx = (src_chip[:, None] * chip_tok_kv + jnp.arange(chip_tok_kv)[None, :]).reshape(span)
    key_seg, key_off = locate(key_idx, starts)
    live = (key_seg[None, :] == row_seg[:, None]) & (key_idx[None, :] <= row_idx[:, None])
    scores = (
        jnp.einsum("rd,nd->rn", query_rows, key_piece, preferred_element_type=jnp.float32) * scale
    )
    scores = jnp.where(live, scores, -1e30)
    new_max = jnp.max(scores, axis=1)
    probs = jnp.where(live, jnp.exp(scores - new_max[:, None]), 0.0)
    new_sum = jnp.sum(probs, axis=1)
    new_weighted = jnp.dot(
        probs.astype(jnp.bfloat16), value_piece, preferred_element_type=jnp.float32
    )
    att_rows = (new_weighted / new_sum[:, None]).astype(jnp.bfloat16)
    chip_att = jnp.concatenate(
        [att_rows[h * chip_tok:(h + 1) * chip_tok] for h in range(groups)], axis=1
    )
    if xor_plan:
        per_c = out_weight.shape[0]

        def part(att, w):
            return jnp.dot(att, w.T, preferred_element_type=jnp.float32).astype(jnp.bfloat16)

        x_pairs = [(i, i ^ 1) for i in range(chips)]
        y_pairs = [(i, i ^ 2) for i in range(chips)]
        att_x = lax.ppermute(chip_att, "chip", x_pairs)
        att_y = lax.ppermute(chip_att, "chip", y_pairs)
        w_x, w_y, att_x, att_y = lax.optimization_barrier((w_x, w_y, att_x, att_y))
        cut = per_c // 2
        back_x = lax.ppermute(part(att_x, w_y[:cut]), "chip", x_pairs)
        back_y = lax.ppermute(part(att_y, w_x[cut:]), "chip", y_pairs)
        diag = jnp.concatenate([back_x, back_y], axis=1)
        by_dist = jnp.stack([part(chip_att, out_weight), part(chip_att, w_x), part(chip_att, w_y), diag])
        here = lax.axis_index("chip")
        routed = jnp.stack(
            [lax.dynamic_index_in_dim(by_dist, here ^ c, 0, keepdims=False) for c in range(kvs)]
        ).reshape(kvs * cores, tok_rows, per_c)
    else:
        per_c = w_share.shape[0] // kvs
        routed = (
            jnp.einsum(
                "ctk,cnk->ctn",
                jnp.broadcast_to(chip_att, (kvs,) + chip_att.shape),
                w_share.reshape(kvs, per_c, w_share.shape[1]),
                preferred_element_type=jnp.float32,
            )
            .astype(jnp.bfloat16)
            .reshape(kvs * cores, tok_rows, per_c)
        )
    got = lax.all_to_all(routed, ("kv", "core"), 0, 0, tiled=True)
    total = jnp.sum(got.reshape(kvs, cores, tok_rows, per_c).astype(jnp.float32), axis=0)
    rows = out_weight.shape[0]
    if per_c == rows:
        hidden = jnp.concatenate([total[k] for k in range(cores)], axis=1).astype(jnp.bfloat16)
    else:
        hidden = (
            total.reshape(cores, tok_rows, per_c // rows, rows)
            .transpose(1, 2, 0, 3)
            .reshape(tok_rows, cores * per_c)
            .astype(jnp.bfloat16)
        )
    return (hidden, rot_keys)


def solution(mesh):
    kv_size, blk_size = mesh.devices.shape
    sub = Mesh(mesh.devices.reshape(kv_size, blk_size // 2, 2), ("kv",) + BLK)
    return jax.shard_map(
        body,
        mesh=sub,
        in_specs=(P(BLK, "kv"), P(BLK, "kv"), P(BLK, "kv"), P(), P(BLK, "kv")),
        out_specs=(P(BLK, "kv"), P(BLK, "kv")),
        check_vma=False,
    )
```

```python
import jax
import jax.numpy as jnp
import numpy as np
from jax import lax
from jax.sharding import Mesh
from jax.sharding import PartitionSpec as P

rope_base = 500000.0
BLK = ("chip", "core")


def locate(index, starts):
    hit = starts[None, :] <= index[:, None]
    segment = jnp.sum(hit.astype(jnp.int32), axis=1) - 1
    offset = jnp.max(jnp.where(hit, starts[None, :], 0), axis=1)
    return (segment, offset)


def half_swap(width, head_size):
    half = head_size // 2
    col = np.arange(width)
    within = col % head_size
    src = np.where(within < half, col + half, col - half)
    sign = np.where(within < half, -1.0, 1.0)
    swap = np.zeros((width, width), np.float32)
    swap[src, col] = sign
    return jnp.asarray(swap, jnp.bfloat16)


def rotate_flat(field, positions, head_size):
    half = head_size // 2
    steps = jnp.arange(half).astype(jnp.float32) * (2.0 / head_size)
    inverse = jnp.power(jnp.float32(rope_base), -steps)
    angle = positions.astype(jnp.float32)[:, None] * inverse[None, :]
    reps = field.shape[1] // head_size
    cosine = jnp.tile(jnp.cos(angle), (1, 2 * reps))
    sine = jnp.tile(jnp.sin(angle), (1, 2 * reps))
    swapped = jnp.dot(
        field, half_swap(field.shape[1], head_size), preferred_element_type=jnp.float32
    )
    return field.astype(jnp.float32) * cosine + swapped * sine


def body(queries, keys, values, lengths, out_weight):
    tok_rows = queries.shape[0]
    head_size = keys.shape[1]
    groups = queries.shape[1] // head_size
    cores = lax.axis_size("core")
    chips = lax.axis_size("chip")
    total_len = tok_rows * chips * cores
    seg_id = jnp.arange(lengths.shape[0] + 1)[:, None]
    short_id = jnp.arange(lengths.shape[0])[None, :]
    tail = jnp.sum(jnp.where(short_id >= seg_id - 1, lengths[None, :], 0), axis=1)
    starts = jnp.where(seg_id[:, 0] == 0, 0, total_len - tail)
    blk_idx = lax.axis_index("chip") * cores + lax.axis_index("core")
    first_tok = blk_idx * tok_rows
    query_idx = first_tok + jnp.arange(tok_rows)
    query_seg, query_off = locate(query_idx, starts)
    positions = query_idx - query_off
    kvs = lax.axis_size("kv")
    xor_plan = chips == 4 and kvs == chips
    if xor_plan:
        w_x = lax.ppermute(out_weight, "chip", [(i, i ^ 1) for i in range(chips)])
        w_y = lax.ppermute(out_weight, "chip", [(i, i ^ 2) for i in range(chips)])
    elif chips <= 8:
        held = [out_weight] + [
            lax.ppermute(out_weight, "chip", [(i, (i + s) % chips) for i in range(chips)])
            for s in range(1, chips)
        ]
        back = jnp.stack(held[::-1] + held[::-1], axis=0)
        here = lax.axis_index("chip")
        w_share = lax.dynamic_slice_in_dim(back, chips - 1 - here, chips, 0).reshape(
            chips * out_weight.shape[0], out_weight.shape[1]
        )
    else:
        w_share = lax.all_gather(out_weight, "chip", axis=0, tiled=True)
    rot_keys = rotate_flat(keys, positions, head_size).astype(jnp.bfloat16)
    rot_queries = rotate_flat(queries, positions, head_size).astype(jnp.bfloat16)
    width = queries.shape[1]
    chip_rows = lax.all_gather(
        jnp.concatenate([rot_queries, rot_keys, values], axis=1), "core", axis=0, tiled=True
    )
    chip_kv = chip_rows[:, width:]
    if chips <= 8:
        kv_pair = jnp.concatenate(
            [chip_kv]
            + [
                lax.ppermute(chip_kv, "chip", [(i, (i + s) % chips) for i in range(chips)])
                for s in range(1, chips)
            ],
            axis=0,
        )
        src_chip = (lax.axis_index("chip") - jnp.arange(chips)) % chips
    else:
        kv_pair = lax.all_gather(chip_kv, "chip", axis=0, tiled=True)
        src_chip = jnp.arange(chips)
    chip_q = chip_rows[:, :width]
    chip_tok = cores * tok_rows
    chip_idx = lax.axis_index("chip") * chip_tok + jnp.arange(chip_tok)
    chip_seg, _ = locate(chip_idx, starts)
    query_rows = jnp.concatenate(
        [chip_q[:, h * head_size:(h + 1) * head_size] for h in range(groups)], axis=0
    )
    row_idx = jnp.tile(chip_idx, groups)
    row_seg = jnp.tile(chip_seg, groups)
    scale = 1.0 / head_size**0.5
    key_piece = kv_pair[:, :head_size]
    value_piece = kv_pair[:, head_size:]
    span = key_piece.shape[0]
    chip_tok_kv = chip_kv.shape[0]
    key_idx = (src_chip[:, None] * chip_tok_kv + jnp.arange(chip_tok_kv)[None, :]).reshape(span)
    key_seg, key_off = locate(key_idx, starts)
    live = (key_seg[None, :] == row_seg[:, None]) & (key_idx[None, :] <= row_idx[:, None])
    scores = (
        jnp.einsum("rd,nd->rn", query_rows, key_piece, preferred_element_type=jnp.float32) * scale
    )
    scores = jnp.where(live, scores, -1e30)
    new_max = jnp.max(scores, axis=1)
    probs = jnp.where(live, jnp.exp(scores - new_max[:, None]), 0.0)
    new_sum = jnp.sum(probs, axis=1)
    new_weighted = jnp.dot(
        probs.astype(jnp.bfloat16), value_piece, preferred_element_type=jnp.float32
    )
    att_rows = (new_weighted / new_sum[:, None]).astype(jnp.bfloat16)
    chip_att = jnp.concatenate(
        [att_rows[h * chip_tok:(h + 1) * chip_tok] for h in range(groups)], axis=1
    )
    if xor_plan:
        per_c = out_weight.shape[0]

        def part(att, w):
            return jnp.dot(att, w.T, preferred_element_type=jnp.float32).astype(jnp.bfloat16)

        att_x = lax.ppermute(chip_att, "chip", [(i, i ^ 1) for i in range(chips)])
        w_x, w_y, att_x = lax.optimization_barrier((w_x, w_y, att_x))
        diag = lax.ppermute(part(att_x, w_y), "chip", [(i, i ^ 1) for i in range(chips)])
        by_dist = jnp.stack([part(chip_att, out_weight), part(chip_att, w_x), part(chip_att, w_y), diag])
        here = lax.axis_index("chip")
        routed = jnp.stack(
            [lax.dynamic_index_in_dim(by_dist, here ^ c, 0, keepdims=False) for c in range(kvs)]
        ).reshape(kvs * cores, tok_rows, per_c)
    else:
        per_c = w_share.shape[0] // kvs
        routed = (
            jnp.einsum(
                "ctk,cnk->ctn",
                jnp.broadcast_to(chip_att, (kvs,) + chip_att.shape),
                w_share.reshape(kvs, per_c, w_share.shape[1]),
                preferred_element_type=jnp.float32,
            )
            .astype(jnp.bfloat16)
            .reshape(kvs * cores, tok_rows, per_c)
        )
    got = lax.all_to_all(routed, ("kv", "core"), 0, 0, tiled=True)
    total = jnp.sum(got.reshape(kvs, cores, tok_rows, per_c).astype(jnp.float32), axis=0)
    rows = out_weight.shape[0]
    if per_c == rows:
        hidden = jnp.concatenate([total[k] for k in range(cores)], axis=1).astype(jnp.bfloat16)
    else:
        hidden = (
            total.reshape(cores, tok_rows, per_c // rows, rows)
            .transpose(1, 2, 0, 3)
            .reshape(tok_rows, cores * per_c)
            .astype(jnp.bfloat16)
        )
    return (hidden, rot_keys)


def solution(mesh):
    kv_size, blk_size = mesh.devices.shape
    sub = Mesh(mesh.devices.reshape(kv_size, blk_size // 2, 2), ("kv",) + BLK)
    return jax.shard_map(
        body,
        mesh=sub,
        in_specs=(P(BLK, "kv"), P(BLK, "kv"), P(BLK, "kv"), P(), P(BLK, "kv")),
        out_specs=(P(BLK, "kv"), P(BLK, "kv")),
        check_vma=False,
    )
```

```python
import jax
import jax.numpy as jnp
import numpy as np
from jax import lax
from jax.sharding import Mesh
from jax.sharding import PartitionSpec as P

rope_base = 500000.0
BLK = ("chip", "core")


def locate(index, starts):
    hit = starts[None, :] <= index[:, None]
    segment = jnp.sum(hit.astype(jnp.int32), axis=1) - 1
    offset = jnp.max(jnp.where(hit, starts[None, :], 0), axis=1)
    return (segment, offset)


def half_swap(width, head_size):
    half = head_size // 2
    col = np.arange(width)
    within = col % head_size
    src = np.where(within < half, col + half, col - half)
    sign = np.where(within < half, -1.0, 1.0)
    swap = np.zeros((width, width), np.float32)
    swap[src, col] = sign
    return jnp.asarray(swap, jnp.bfloat16)


def rotate_flat(field, positions, head_size):
    half = head_size // 2
    steps = jnp.arange(half).astype(jnp.float32) * (2.0 / head_size)
    inverse = jnp.power(jnp.float32(rope_base), -steps)
    angle = positions.astype(jnp.float32)[:, None] * inverse[None, :]
    reps = field.shape[1] // head_size
    cosine = jnp.tile(jnp.cos(angle), (1, 2 * reps))
    sine = jnp.tile(jnp.sin(angle), (1, 2 * reps))
    swapped = jnp.dot(
        field, half_swap(field.shape[1], head_size), preferred_element_type=jnp.float32
    )
    return field.astype(jnp.float32) * cosine + swapped * sine


def body(queries, keys, values, lengths, out_weight):
    tok_rows = queries.shape[0]
    head_size = keys.shape[1]
    groups = queries.shape[1] // head_size
    cores = lax.axis_size("core")
    chips = lax.axis_size("chip")
    total_len = tok_rows * chips * cores
    seg_id = jnp.arange(lengths.shape[0] + 1)[:, None]
    short_id = jnp.arange(lengths.shape[0])[None, :]
    tail = jnp.sum(jnp.where(short_id >= seg_id - 1, lengths[None, :], 0), axis=1)
    starts = jnp.where(seg_id[:, 0] == 0, 0, total_len - tail)
    blk_idx = lax.axis_index("chip") * cores + lax.axis_index("core")
    first_tok = blk_idx * tok_rows
    query_idx = first_tok + jnp.arange(tok_rows)
    query_seg, query_off = locate(query_idx, starts)
    positions = query_idx - query_off
    kvs = lax.axis_size("kv")
    xor_plan = chips == 4 and kvs == chips
    if xor_plan:
        w_x = lax.ppermute(out_weight, "chip", [(i, i ^ 1) for i in range(chips)])
        w_y = lax.ppermute(out_weight, "chip", [(i, i ^ 2) for i in range(chips)])
    elif chips <= 8:
        held = [out_weight] + [
            lax.ppermute(out_weight, "chip", [(i, (i + s) % chips) for i in range(chips)])
            for s in range(1, chips)
        ]
        back = jnp.stack(held[::-1] + held[::-1], axis=0)
        here = lax.axis_index("chip")
        w_share = lax.dynamic_slice_in_dim(back, chips - 1 - here, chips, 0).reshape(
            chips * out_weight.shape[0], out_weight.shape[1]
        )
    else:
        w_share = lax.all_gather(out_weight, "chip", axis=0, tiled=True)
    rot_keys = rotate_flat(keys, positions, head_size).astype(jnp.bfloat16)
    rot_queries = rotate_flat(queries, positions, head_size).astype(jnp.bfloat16)
    width = queries.shape[1]
    chip_rows = lax.all_gather(
        jnp.concatenate([rot_queries, rot_keys, values], axis=1), "core", axis=0, tiled=True
    )
    chip_kv = chip_rows[:, width:]
    if chips <= 8:
        reach = chips // 2
        mine = [list(range(1, reach + 1)), [chips - p for p in range(1, reach + 1)]]
        fetched = []
        for p in range(reach):
            pairs = []
            for i in range(chips):
                for k in range(cores):
                    pairs.append((i * cores + k, ((i + mine[k][p]) % chips) * cores + k))
            fetched.append(lax.ppermute(chip_kv, BLK, pairs))
        both = lax.all_gather(jnp.stack(fetched, 0), "core", axis=0, tiled=False)
        pieces = {0: chip_kv}
        for k in range(cores):
            for p in range(reach):
                pieces.setdefault(mine[k][p], both[k, p])
        kv_pair = jnp.concatenate([pieces[s] for s in range(chips)], axis=0)
        src_chip = (lax.axis_index("chip") - jnp.arange(chips)) % chips
    else:
        kv_pair = lax.all_gather(chip_kv, "chip", axis=0, tiled=True)
        src_chip = jnp.arange(chips)
    chip_q = chip_rows[:, :width]
    chip_tok = cores * tok_rows
    chip_idx = lax.axis_index("chip") * chip_tok + jnp.arange(chip_tok)
    chip_seg, _ = locate(chip_idx, starts)
    query_rows = jnp.concatenate(
        [chip_q[:, h * head_size:(h + 1) * head_size] for h in range(groups)], axis=0
    )
    row_idx = jnp.tile(chip_idx, groups)
    row_seg = jnp.tile(chip_seg, groups)
    scale = 1.0 / head_size**0.5
    key_piece = kv_pair[:, :head_size]
    value_piece = kv_pair[:, head_size:]
    span = key_piece.shape[0]
    chip_tok_kv = chip_kv.shape[0]
    key_idx = (src_chip[:, None] * chip_tok_kv + jnp.arange(chip_tok_kv)[None, :]).reshape(span)
    key_seg, key_off = locate(key_idx, starts)
    live = (key_seg[None, :] == row_seg[:, None]) & (key_idx[None, :] <= row_idx[:, None])
    scores = (
        jnp.einsum("rd,nd->rn", query_rows, key_piece, preferred_element_type=jnp.float32) * scale
    )
    scores = jnp.where(live, scores, -1e30)
    new_max = jnp.max(scores, axis=1)
    probs = jnp.where(live, jnp.exp(scores - new_max[:, None]), 0.0)
    new_sum = jnp.sum(probs, axis=1)
    new_weighted = jnp.dot(
        probs.astype(jnp.bfloat16), value_piece, preferred_element_type=jnp.float32
    )
    att_rows = (new_weighted / new_sum[:, None]).astype(jnp.bfloat16)
    chip_att = jnp.concatenate(
        [att_rows[h * chip_tok:(h + 1) * chip_tok] for h in range(groups)], axis=1
    )
    if xor_plan:
        per_c = out_weight.shape[0]

        def part(att, w):
            return jnp.dot(att, w.T, preferred_element_type=jnp.float32).astype(jnp.bfloat16)

        att_y = lax.ppermute(chip_att, "chip", [(i, i ^ 2) for i in range(chips)])
        w_x, w_y, att_y = lax.optimization_barrier((w_x, w_y, att_y))
        diag = lax.ppermute(part(att_y, w_x), "chip", [(i, i ^ 2) for i in range(chips)])
        by_dist = jnp.stack([part(chip_att, out_weight), part(chip_att, w_x), part(chip_att, w_y), diag])
        here = lax.axis_index("chip")
        routed = jnp.stack(
            [lax.dynamic_index_in_dim(by_dist, here ^ c, 0, keepdims=False) for c in range(kvs)]
        ).reshape(kvs * cores, tok_rows, per_c)
    else:
        per_c = w_share.shape[0] // kvs
        routed = (
            jnp.einsum(
                "ctk,cnk->ctn",
                jnp.broadcast_to(chip_att, (kvs,) + chip_att.shape),
                w_share.reshape(kvs, per_c, w_share.shape[1]),
                preferred_element_type=jnp.float32,
            )
            .astype(jnp.bfloat16)
            .reshape(kvs * cores, tok_rows, per_c)
        )
    got = lax.all_to_all(routed, ("kv", "core"), 0, 0, tiled=True)
    total = jnp.sum(got.reshape(kvs, cores, tok_rows, per_c).astype(jnp.float32), axis=0)
    rows = out_weight.shape[0]
    if per_c == rows:
        hidden = jnp.concatenate([total[k] for k in range(cores)], axis=1).astype(jnp.bfloat16)
    else:
        hidden = (
            total.reshape(cores, tok_rows, per_c // rows, rows)
            .transpose(1, 2, 0, 3)
            .reshape(tok_rows, cores * per_c)
            .astype(jnp.bfloat16)
        )
    return (hidden, rot_keys)


def solution(mesh):
    kv_size, blk_size = mesh.devices.shape
    sub = Mesh(mesh.devices.reshape(kv_size, blk_size // 2, 2), ("kv",) + BLK)
    return jax.shard_map(
        body,
        mesh=sub,
        in_specs=(P(BLK, "kv"), P(BLK, "kv"), P(BLK, "kv"), P(), P(BLK, "kv")),
        out_specs=(P(BLK, "kv"), P(BLK, "kv")),
        check_vma=False,
    )
```
